256 devices in a mesh: ctx: 128 (over y, x, z), head: 2 (over core).
Axes of the slice: x: 4, y: 4, z: 8, core: 2. Of those that a mesh axis runs over, the one named last changes fastest.
Arguments:
- queries: bfloat16 [16384, 4096], P('ctx', 'head'), may hold values from -9 to 9
- key_rows: bfloat16 [16384, 4096], P('ctx', 'head'), may hold values from -9 to 9
- value_rows: bfloat16 [16384, 4096], P('ctx', 'head'), may hold values from -6 to 6
- offsets: int32 [3, 32], P(None, 'head'), may hold values from 0 to 3, as said below
- sublayer_norm_gain: float32 [4096], P('head'), may hold values from 0.25 to 1.75
- cotangent: bfloat16 [16384, 4096], P('ctx', 'head'), may hold values from -6 to 6
Outputs:
- normed: bfloat16 [16384, 4096], P('ctx', 'head')
- query_grad: bfloat16 [16384, 4096], P('ctx', 'head')
- key_grad: bfloat16 [16384, 4096], P('ctx', 'head')
- value_grad: bfloat16 [16384, 4096], P('ctx', 'head')
The draws below stay inside these ranges and needn't reach their ends.
Inputs may be any that keep to these rules, and one draw needn't show every extreme that they name: Row l holds offsets of 0 to 2**l - 1, and each of these values belongs to exactly 32 / 2**l heads.
All inputs are finite; a program needn't handle non-finite values.
Results may differ from the reference program's by a relative error of at most 0.007.
Values may be sent and summed in bfloat16 or wider, within the bound.
No kernel may reach another device: no remote copies, remote signals or barrier semaphores. Data moves between devices by JAX's collectives and lax.ppermute only.
A program may use at most 192 MiB of HBM per device.

```python
import math
from functools import reduce
import jax
import jax.numpy as jnp
from jax import lax

HEADS = 32
HD = 128
SEG0 = 512
LEVELS = 3
TOKENS = 16384
FEATURES = 4096


def draw_pair(key):
    base = jax.random.fold_in(key, 11)
    key_query, key_keys = jax.random.split(base, 2)
    shape3 = (TOKENS, HEADS, HD)
    query_vals = jnp.clip(jax.random.normal(key_query, shape3, jnp.float32), -4.0, 4.0)
    keys_vals = jnp.clip(jax.random.normal(key_keys, shape3, jnp.float32), -4.0, 4.0)
    query_out = query_vals.reshape(TOKENS, HEADS * HD).astype(jnp.bfloat16)
    keys_out = keys_vals.reshape(TOKENS, HEADS * HD).astype(jnp.bfloat16)
    return (query_out, keys_out)


def draw_queries(key, part):
    return draw_pair(key)[0]


def draw_key_rows(key, part):
    return draw_pair(key)[1]


def draw_offsets(key, part):
    levels_out = []
    for level_num in range(LEVELS):
        sub_key = jax.random.fold_in(key, 100 + level_num)
        order = jax.random.permutation(sub_key, HEADS).astype(jnp.int32)
        shifted = jax.random.randint(jax.random.fold_in(sub_key, 1), (), 0, 2 ** level_num)
        levels_out.append((order + shifted) % 2 ** level_num)
    return jnp.stack(levels_out).astype(jnp.int32)


def level_of(stream_key, shape, cuts, least, high):
    def one(axis_at, blocks):
        steps = jax.random.uniform(jax.random.fold_in(jax.random.fold_in(stream_key, 6), axis_at), (blocks,), jnp.float32, least / len(cuts), high / len(cuts))
        return jnp.repeat(jnp.exp(steps), shape[axis_at] // blocks).reshape((-1,) + (1,) * (len(shape) - axis_at - 1))

    factor_of = one(*cuts[0])
    for cut in cuts[1:]:
        factor_of = factor_of * one(*cut)
    return factor_of


def scatter_about(rng, extent, width, bound, pieces=(), kind=jnp.bfloat16):
    entries = jax.random.normal(rng, extent, jnp.float32) * width
    if len(pieces) > 0:
        entries = level_of(rng, extent, pieces, -0.22, 0.18) * entries
    return jnp.clip(entries, min=-bound, max=bound).astype(kind)


def setup_inputs(seed: int = 0) -> dict:
    key_list = jax.random.split(jax.random.key(seed), 7)
    return {
        "queries": draw_queries(jax.random.fold_in(key_list[6], 71), 0),
        "key_rows": draw_key_rows(jax.random.fold_in(key_list[6], 71), 0),
        "value_rows": scatter_about(key_list[2], (TOKENS, FEATURES), 1.0, 6.0, ((0, 128), (1, 2))),
        "offsets": draw_offsets(jax.random.fold_in(key_list[6], 71), 0),
        "sublayer_norm_gain": jnp.clip(1.0 + 0.15 * jax.random.normal(key_list[4], (FEATURES,), jnp.float32), 0.25, 1.75),
        "cotangent": scatter_about(key_list[5], (TOKENS, FEATURES), 1.0, 6.0, ((0, 128), (1, 2))),
    }


NEG_FILL = -1e+30
EPSILON = 1e-05

def pick_rows(source, offset, stride):
    shaped = source.reshape((source.shape[0] // stride, stride) + source.shape[1:])
    return lax.dynamic_index_in_dim(shaped, offset, axis=1, keepdims=False)

def put_rows(picked, offset, stride, filler):
    count = picked.shape[0]
    chosen = jnp.arange(stride, dtype=jnp.int32) == offset
    chosen = chosen.reshape((1, stride) + (1,) * (picked.ndim - 1))
    spread = jnp.where(chosen, picked[:, None], jnp.asarray(filler, picked.dtype))
    return spread.reshape((count * stride,) + picked.shape[1:])

def round_trip(values):
    return lax.optimization_barrier(values.astype(jnp.bfloat16)).astype(jnp.float32)

def head_forward(operands):
    query_head, key_head, value_head, head_offsets = operands
    score_scale = 1.0 / math.sqrt(HD)
    maxima = []
    totals = []
    partials = []
    for level_num in range(LEVELS):
        stride = 2 ** level_num
        offset = head_offsets[level_num]
        query_sel = pick_rows(query_head, offset, stride).reshape(-1, SEG0, HD).astype(jnp.float32)
        key_sel = pick_rows(key_head, offset, stride).reshape(-1, SEG0, HD).astype(jnp.float32)
        value_sel = pick_rows(value_head, offset, stride).reshape(-1, SEG0, HD).astype(jnp.float32)
        scores = jnp.einsum('sqd,skd->sqk', query_sel, key_sel) * score_scale
        row_max = lax.optimization_barrier(jnp.max(scores, axis=-1))
        weights = jnp.exp(scores - row_max[..., None])
        row_total = lax.optimization_barrier(jnp.sum(weights, axis=-1))
        level_out = jnp.einsum('sqk,skd->sqd', round_trip(weights), value_sel)
        maxima.append(put_rows(row_max.reshape(-1), offset, stride, NEG_FILL))
        totals.append(put_rows(row_total.reshape(-1), offset, stride, 0.0))
        partials.append(put_rows(level_out.reshape(-1, HD), offset, stride, 0.0))
    top_max = reduce(jnp.maximum, maxima)
    factors = [jnp.exp(each_max - top_max) for each_max in maxima]
    total = factors[0] * totals[0]
    summed = factors[0][:, None] * partials[0]
    for level_num in range(1, LEVELS):
        total = total + factors[level_num] * totals[level_num]
        summed = summed + factors[level_num][:, None] * partials[level_num]
    attended = (summed / total[:, None]).astype(jnp.bfloat16)
    return (attended, top_max + jnp.log(total))

def head_backward(operands):
    query_head, key_head, value_head, dout_head, lse_head, delta_head, head_offsets = operands
    score_scale = 1.0 / math.sqrt(HD)
    query_acc = jnp.zeros((TOKENS, HD), jnp.float32)
    key_acc = jnp.zeros((TOKENS, HD), jnp.float32)
    value_acc = jnp.zeros((TOKENS, HD), jnp.float32)
    for level_num in range(LEVELS):
        stride = 2 ** level_num
        offset = head_offsets[level_num]
        query_sel = pick_rows(query_head, offset, stride).reshape(-1, SEG0, HD).astype(jnp.float32)
        key_sel = pick_rows(key_head, offset, stride).reshape(-1, SEG0, HD).astype(jnp.float32)
        value_sel = pick_rows(value_head, offset, stride).reshape(-1, SEG0, HD).astype(jnp.float32)
        dout_sel = pick_rows(dout_head, offset, stride).reshape(-1, SEG0, HD).astype(jnp.float32)
        lse_sel = pick_rows(lse_head, offset, stride).reshape(-1, SEG0)
        delta_sel = pick_rows(delta_head, offset, stride).reshape(-1, SEG0)
        scores = jnp.einsum('sqd,skd->sqk', query_sel, key_sel) * score_scale
        probs = jnp.exp(scores - lse_sel[..., None])
        value_part = jnp.einsum('sqk,sqd->skd', round_trip(probs), dout_sel)
        dprobs = jnp.einsum('sqd,skd->sqk', dout_sel, value_sel)
        dscores = round_trip(probs * (dprobs - delta_sel[..., None]))
        query_part = jnp.einsum('sqk,skd->sqd', dscores, key_sel) * score_scale
        key_part = jnp.einsum('sqk,sqd->skd', dscores, query_sel) * score_scale
        query_acc = query_acc + put_rows(query_part.reshape(-1, HD), offset, stride, 0.0)
        key_acc = key_acc + put_rows(key_part.reshape(-1, HD), offset, stride, 0.0)
        value_acc = value_acc + put_rows(value_part.reshape(-1, HD), offset, stride, 0.0)
    return (query_acc.astype(jnp.bfloat16), key_acc.astype(jnp.bfloat16), value_acc.astype(jnp.bfloat16))

def by_head(array):
    return array.reshape(TOKENS, HEADS, HD).transpose(1, 0, 2)

def from_heads(array):
    return array.transpose(1, 0, 2).reshape(TOKENS, HEADS * HD)

def reference(queries, key_rows, value_rows, offsets, sublayer_norm_gain, cotangent):
    feature_total_count = HEADS * HD
    query_heads = by_head(queries)
    key_heads = by_head(key_rows)
    value_heads = by_head(value_rows)
    head_offsets = offsets.T
    attended, log_total = lax.map(head_forward, (query_heads, key_heads, value_heads, head_offsets))
    attended_rows_flattened = from_heads(attended).astype(jnp.float32)
    feature_mean = lax.optimization_barrier(jnp.sum(attended_rows_flattened, axis=1)) / feature_total_count
    variance = lax.optimization_barrier(jnp.sum(attended_rows_flattened * attended_rows_flattened, axis=1)) / feature_total_count - feature_mean * feature_mean
    inverse_deviation = 1.0 / jnp.sqrt(variance + EPSILON)
    normalized_input = (attended_rows_flattened - feature_mean[:, None]) * inverse_deviation[:, None]
    normed = (normalized_input * sublayer_norm_gain[None, :]).astype(jnp.bfloat16)
    normalized_gradient = cotangent.astype(jnp.float32) * sublayer_norm_gain[None, :]
    gradient_sum_first = lax.optimization_barrier(jnp.sum(normalized_gradient, axis=1))
    gradient_sum_second = lax.optimization_barrier(jnp.sum(normalized_gradient * normalized_input, axis=1))
    attended_gradient = ((normalized_gradient - gradient_sum_first[:, None] / feature_total_count - normalized_input * gradient_sum_second[:, None] / feature_total_count) * inverse_deviation[:, None]).astype(jnp.bfloat16)
    dout_heads = by_head(attended_gradient)
    delta = lax.optimization_barrier(jnp.sum(dout_heads.astype(jnp.float32) * attended.astype(jnp.float32), axis=-1))
    grads = lax.map(head_backward, (query_heads, key_heads, value_heads, dout_heads, log_total, delta, head_offsets))
    return (normed, from_heads(grads[0]), from_heads(grads[1]), from_heads(grads[2]))
```

```python
from functools import partial, reduce
import math

import jax
import jax.numpy as jnp
from jax import lax
from jax.sharding import PartitionSpec as P

SEG0 = 512


NEG_FILL = -1e30
EPSILON = 1e-05


def pick_rows(source, mask_table, stride):
    count = source.shape[0] // stride
    shaped = source.reshape((count, stride) + source.shape[1:])
    chosen = mask_table.reshape((1, stride, mask_table.shape[1]) + (1,) * (source.ndim - 2))
    return jnp.sum(jnp.where(chosen, shaped, jnp.zeros((), source.dtype)), axis=1)


def put_rows(picked, mask_table, stride, filler):
    chosen = mask_table.reshape((1, stride, mask_table.shape[1]) + (1,) * (picked.ndim - 2))
    spread = jnp.where(chosen, picked[:, None], jnp.asarray(filler, picked.dtype))
    return spread.reshape((picked.shape[0] * stride,) + picked.shape[1:])


def gather_group(members, group_axes):
    if not group_axes:
        return members
    return tuple(lax.all_gather(part, group_axes, axis=0, tiled=True) for part in members)


def grad_block(
    query_seg, key_seg, value_seg, dout_seg, lse_seg, delta_seg, score_scale, want_query, want_keys
):
    lse_t = jnp.transpose(lse_seg, (0, 2, 1))[..., None]
    delta_t = jnp.transpose(delta_seg, (0, 2, 1))[..., None]
    scores = (
        jnp.einsum("sqhd,skhd->shqk", query_seg, key_seg, preferred_element_type=jnp.float32)
        * score_scale
    )
    probs = jnp.exp(scores - lse_t)
    dprobs = jnp.einsum("sqhd,skhd->shqk", dout_seg, value_seg, preferred_element_type=jnp.float32)
    dscores = (probs * (dprobs - delta_t)).astype(jnp.bfloat16)
    query_part = None
    key_part = None
    value_part = None
    if want_query:
        query_part = (
            jnp.einsum("shqk,skhd->sqhd", dscores, key_seg, preferred_element_type=jnp.float32)
            * score_scale
        )
    if want_keys:
        probs_half = probs.astype(jnp.bfloat16)
        key_part = (
            jnp.einsum("shqk,sqhd->skhd", dscores, query_seg, preferred_element_type=jnp.float32)
            * score_scale
        )
        value_part = jnp.einsum(
            "shqk,sqhd->skhd", probs_half, dout_seg, preferred_element_type=jnp.float32
        )
    return (query_part, key_part, value_part)


def on_device(queries, key_rows, value_rows, offsets, sublayer_norm_gain, cotangent, level_axes):
    tok_rows = queries.shape[0]
    head_local = offsets.shape[1]
    head_size = queries.shape[1] // head_local
    level_count = offsets.shape[0]
    feature_total_count = lax.axis_size("head") * queries.shape[1]
    score_scale = 1.0 / math.sqrt(head_size)
    shape3 = (tok_rows, head_local, head_size)
    query_all = queries.reshape(shape3)
    key_all = key_rows.reshape(shape3)
    value_all = value_rows.reshape(shape3)

    def level_layout(level_num):
        stride = 2**level_num
        picked_rows = tok_rows // stride
        group_bits = level_axes[level_num]
        seg_count = max(1, picked_rows // SEG0)
        mask_table = jnp.arange(stride, dtype=jnp.int32)[:, None] == offsets[level_num][None, :]
        return (stride, picked_rows, group_bits, seg_count, mask_table)

    stored = []
    maxima = []
    totals = []
    partials = []
    for level_num in range(level_count):
        stride, picked_rows, group_bits, seg_count, mask_table = level_layout(level_num)
        query_sel = pick_rows(query_all, mask_table, stride)
        key_sel = pick_rows(key_all, mask_table, stride)
        value_sel = pick_rows(value_all, mask_table, stride)
        key_group, value_group = gather_group((key_sel, value_sel), group_bits)
        stored.append((key_group, value_group))
        query_seg = query_sel.reshape(seg_count, -1, head_local, head_size)
        key_seg = key_group.reshape(seg_count, SEG0, head_local, head_size)
        value_seg = value_group.reshape(seg_count, SEG0, head_local, head_size)
        scores = (
            jnp.einsum("sqhd,skhd->shqk", query_seg, key_seg, preferred_element_type=jnp.float32)
            * score_scale
        )
        row_max = jnp.max(scores, axis=-1)
        weights = jnp.exp(scores - row_max[..., None])
        row_total = jnp.sum(weights, axis=-1)
        level_out = jnp.einsum(
            "shqk,skhd->sqhd",
            weights.astype(jnp.bfloat16),
            value_seg,
            preferred_element_type=jnp.float32,
        )
        flat_max = jnp.transpose(row_max, (0, 2, 1)).reshape(picked_rows, head_local)
        flat_total = jnp.transpose(row_total, (0, 2, 1)).reshape(picked_rows, head_local)
        maxima.append(put_rows(flat_max, mask_table, stride, NEG_FILL))
        totals.append(put_rows(flat_total, mask_table, stride, 0.0))
        partials.append(
            put_rows(level_out.reshape(picked_rows, head_local, head_size), mask_table, stride, 0.0)
        )
    top_max = reduce(jnp.maximum, maxima)
    factors = [jnp.exp(each_max - top_max) for each_max in maxima]
    total = factors[0] * totals[0]
    summed = factors[0][..., None] * partials[0]
    for level_num in range(1, level_count):
        total = total + factors[level_num] * totals[level_num]
        summed = summed + factors[level_num][..., None] * partials[level_num]
    attended = (summed / total[..., None]).astype(jnp.bfloat16)
    log_total = top_max + jnp.log(total)
    attended_rows_flattened = attended.reshape(tok_rows, -1).astype(jnp.float32)
    first_sum, second_sum = lax.psum(
        (
            jnp.sum(attended_rows_flattened, axis=1),
            jnp.sum(attended_rows_flattened * attended_rows_flattened, axis=1),
        ),
        "head",
    )
    feature_mean = first_sum / feature_total_count
    variance = second_sum / feature_total_count - feature_mean * feature_mean
    inverse_deviation = 1.0 / jnp.sqrt(variance + EPSILON)
    normalized_input = (attended_rows_flattened - feature_mean[:, None]) * inverse_deviation[
        :, None
    ]
    normed = (normalized_input * sublayer_norm_gain[None, :]).astype(jnp.bfloat16)
    normalized_gradient = cotangent.astype(jnp.float32) * sublayer_norm_gain[None, :]
    gradient_sum_first, gradient_sum_second = lax.psum(
        (
            jnp.sum(normalized_gradient, axis=1),
            jnp.sum(normalized_gradient * normalized_input, axis=1),
        ),
        "head",
    )
    attended_gradient = (
        (
            normalized_gradient
            - gradient_sum_first[:, None] / feature_total_count
            - normalized_input * gradient_sum_second[:, None] / feature_total_count
        )
        * inverse_deviation[:, None]
    ).astype(jnp.bfloat16)
    dout_all = attended_gradient.reshape(shape3)
    delta = jnp.sum(dout_all.astype(jnp.float32) * attended.astype(jnp.float32), axis=-1)
    query_acc = jnp.zeros(shape3, jnp.float32)
    key_acc = jnp.zeros(shape3, jnp.float32)
    value_acc = jnp.zeros(shape3, jnp.float32)
    for level_num in range(level_count):
        stride, picked_rows, group_bits, seg_count, mask_table = level_layout(level_num)
        query_sel = pick_rows(query_all, mask_table, stride)
        key_sel = pick_rows(key_all, mask_table, stride)
        value_sel = pick_rows(value_all, mask_table, stride)
        dout_sel = pick_rows(dout_all, mask_table, stride)
        lse_sel = pick_rows(log_total, mask_table, stride)
        delta_sel = pick_rows(delta, mask_table, stride)
        key_group, value_group = stored[level_num]
        query_seg = query_sel.reshape(seg_count, -1, head_local, head_size)
        dout_seg = dout_sel.reshape(seg_count, -1, head_local, head_size)
        lse_seg = lse_sel.reshape(seg_count, -1, head_local)
        delta_seg = delta_sel.reshape(seg_count, -1, head_local)
        key_seg = key_group.reshape(seg_count, SEG0, head_local, head_size)
        value_seg = value_group.reshape(seg_count, SEG0, head_local, head_size)
        query_part, unused_key, unused_value = grad_block(
            query_seg, key_seg, value_seg, dout_seg, lse_seg, delta_seg, score_scale, True, False
        )
        query_group, dout_group, lse_group, delta_group = gather_group(
            (query_sel, dout_sel, lse_sel, delta_sel), group_bits
        )
        unused_query, key_part, value_part = grad_block(
            query_group.reshape(seg_count, SEG0, head_local, head_size),
            key_sel.reshape(seg_count, -1, head_local, head_size),
            value_sel.reshape(seg_count, -1, head_local, head_size),
            dout_group.reshape(seg_count, SEG0, head_local, head_size),
            lse_group.reshape(seg_count, SEG0, head_local),
            delta_group.reshape(seg_count, SEG0, head_local),
            score_scale,
            False,
            True,
        )
        key_own = key_part.reshape(picked_rows, head_local, head_size)
        value_own = value_part.reshape(picked_rows, head_local, head_size)
        query_acc = query_acc + put_rows(
            query_part.reshape(picked_rows, head_local, head_size), mask_table, stride, 0.0
        )
        key_acc = key_acc + put_rows(key_own, mask_table, stride, 0.0)
        value_acc = value_acc + put_rows(value_own, mask_table, stride, 0.0)
    flat_shape = (tok_rows, head_local * head_size)
    query_grad = query_acc.astype(jnp.bfloat16).reshape(flat_shape)
    key_grad = key_acc.astype(jnp.bfloat16).reshape(flat_shape)
    value_grad = value_acc.astype(jnp.bfloat16).reshape(flat_shape)
    return (normed, query_grad, key_grad, value_grad)


def split_mesh(mesh, tok_rows, level_count):
    ctx_count = mesh.shape["ctx"]
    sizes = sorted({max(1, SEG0 * 2**level_num // tok_rows) for level_num in range(level_count)})
    factors = []
    done = 1
    for size in sizes:
        if size > done:
            factors.append(size // done)
            done = size
    factors.append(ctx_count // done)
    names = tuple(f"c{index}" for index in range(len(factors)))
    shape = tuple(reversed(factors)) + (mesh.shape["head"],)
    sub_mesh = jax.sharding.Mesh(
        mesh.devices.reshape(shape), tuple(reversed(names)) + ("head",)
    )
    level_axes = []
    for level_num in range(level_count):
        size = max(1, SEG0 * 2**level_num // tok_rows)
        count = 0
        span = 1
        while span < size:
            span *= factors[count]
            count += 1
        level_axes.append(tuple(reversed(names[:count])))
    return sub_mesh, tuple(reversed(names)), level_axes


def solution(mesh):
    def run(queries, key_rows, value_rows, offsets, sublayer_norm_gain, cotangent):
        tok_rows = queries.shape[0] // mesh.shape["ctx"]
        sub_mesh, ctx_axes, level_axes = split_mesh(mesh, tok_rows, offsets.shape[0])
        rows = P(ctx_axes, "head")
        in_specs = (rows, rows, rows, P(None, "head"), P("head"), rows)
        out_specs = (rows, rows, rows, rows)
        body = partial(on_device, level_axes=level_axes)
        return jax.shard_map(
            body, mesh=sub_mesh, in_specs=in_specs, out_specs=out_specs, check_vma=False
        )(queries, key_rows, value_rows, offsets, sublayer_norm_gain, cotangent)

    return run
```

```python
from functools import partial, reduce
import math

import jax
import jax.numpy as jnp
from jax import lax
from jax.sharding import PartitionSpec as P

SEG0 = 512


NEG_FILL = -1e30
EPSILON = 1e-05


def pick_rows(source, mask_table, stride):
    count = source.shape[0] // stride
    shaped = source.reshape((count, stride) + source.shape[1:])
    chosen = mask_table.reshape((1, stride, mask_table.shape[1]) + (1,) * (source.ndim - 2))
    return jnp.sum(jnp.where(chosen, shaped, jnp.zeros((), source.dtype)), axis=1)


def put_rows(picked, mask_table, stride, filler):
    chosen = mask_table.reshape((1, stride, mask_table.shape[1]) + (1,) * (picked.ndim - 2))
    spread = jnp.where(chosen, picked[:, None], jnp.asarray(filler, picked.dtype))
    return spread.reshape((picked.shape[0] * stride,) + picked.shape[1:])


def gather_group(members, group_axes):
    if not group_axes:
        return members
    size = 1
    for name in group_axes:
        size *= lax.axis_size(name)
    stacked = jnp.stack(members, axis=1)
    parts = [stacked]
    for step in range(1, size):
        parts.append(lax.ppermute(stacked, group_axes, [(low, low ^ step) for low in range(size)]))
    whole = jnp.concatenate(parts, 0)
    return tuple(whole[:, index] for index in range(len(members)))


def grad_block(
    query_seg, key_seg, value_seg, dout_seg, lse_seg, delta_seg, score_scale, want_query, want_keys
):
    lse_t = jnp.transpose(lse_seg, (0, 2, 1))[..., None]
    delta_t = jnp.transpose(delta_seg, (0, 2, 1))[..., None]
    scores = (
        jnp.einsum("sqhd,skhd->shqk", query_seg, key_seg, preferred_element_type=jnp.float32)
        * score_scale
    )
    probs = jnp.exp(scores - lse_t)
    dprobs = jnp.einsum("sqhd,skhd->shqk", dout_seg, value_seg, preferred_element_type=jnp.float32)
    dscores = (probs * (dprobs - delta_t)).astype(jnp.bfloat16)
    query_part = None
    key_part = None
    value_part = None
    if want_query:
        query_part = (
            jnp.einsum("shqk,skhd->sqhd", dscores, key_seg, preferred_element_type=jnp.float32)
            * score_scale
        )
    if want_keys:
        probs_half = probs.astype(jnp.bfloat16)
        key_part = (
            jnp.einsum("shqk,sqhd->skhd", dscores, query_seg, preferred_element_type=jnp.float32)
            * score_scale
        )
        value_part = jnp.einsum(
            "shqk,sqhd->skhd", probs_half, dout_seg, preferred_element_type=jnp.float32
        )
    return (query_part, key_part, value_part)


def on_device(queries, key_rows, value_rows, offsets, sublayer_norm_gain, cotangent, level_axes):
    tok_rows = queries.shape[0]
    head_local = offsets.shape[1]
    head_size = queries.shape[1] // head_local
    level_count = offsets.shape[0]
    feature_total_count = lax.axis_size("head") * queries.shape[1]
    score_scale = 1.0 / math.sqrt(head_size)
    shape3 = (tok_rows, head_local, head_size)
    query_all = queries.reshape(shape3)
    key_all = key_rows.reshape(shape3)
    value_all = value_rows.reshape(shape3)

    def level_layout(level_num):
        stride = 2**level_num
        picked_rows = tok_rows // stride
        group_bits = level_axes[level_num]
        seg_count = max(1, picked_rows // SEG0)
        mask_table = jnp.arange(stride, dtype=jnp.int32)[:, None] == offsets[level_num][None, :]
        return (stride, picked_rows, group_bits, seg_count, mask_table)

    stored = []
    maxima = []
    totals = []
    partials = []
    for level_num in range(level_count):
        stride, picked_rows, group_bits, seg_count, mask_table = level_layout(level_num)
        query_sel = pick_rows(query_all, mask_table, stride)
        key_sel = pick_rows(key_all, mask_table, stride)
        value_sel = pick_rows(value_all, mask_table, stride)
        key_group, value_group = gather_group((key_sel, value_sel), group_bits)
        stored.append((key_group, value_group))
        query_seg = query_sel.reshape(seg_count, -1, head_local, head_size)
        key_seg = key_group.reshape(seg_count, SEG0, head_local, head_size)
        value_seg = value_group.reshape(seg_count, SEG0, head_local, head_size)
        scores = (
            jnp.einsum("sqhd,skhd->shqk", query_seg, key_seg, preferred_element_type=jnp.float32)
            * score_scale
        )
        row_max = jnp.max(scores, axis=-1)
        weights = jnp.exp(scores - row_max[..., None])
        row_total = jnp.sum(weights, axis=-1)
        level_out = jnp.einsum(
            "shqk,skhd->sqhd",
            weights.astype(jnp.bfloat16),
            value_seg,
            preferred_element_type=jnp.float32,
        )
        flat_max = jnp.transpose(row_max, (0, 2, 1)).reshape(picked_rows, head_local)
        flat_total = jnp.transpose(row_total, (0, 2, 1)).reshape(picked_rows, head_local)
        maxima.append(put_rows(flat_max, mask_table, stride, NEG_FILL))
        totals.append(put_rows(flat_total, mask_table, stride, 0.0))
        partials.append(
            put_rows(level_out.reshape(picked_rows, head_local, head_size), mask_table, stride, 0.0)
        )
    top_max = reduce(jnp.maximum, maxima)
    factors = [jnp.exp(each_max - top_max) for each_max in maxima]
    total = factors[0] * totals[0]
    summed = factors[0][..., None] * partials[0]
    for level_num in range(1, level_count):
        total = total + factors[level_num] * totals[level_num]
        summed = summed + factors[level_num][..., None] * partials[level_num]
    attended = (summed / total[..., None]).astype(jnp.bfloat16)
    log_total = top_max + jnp.log(total)
    attended_rows_flattened = attended.reshape(tok_rows, -1).astype(jnp.float32)
    first_sum, second_sum = lax.psum(
        (
            jnp.sum(attended_rows_flattened, axis=1),
            jnp.sum(attended_rows_flattened * attended_rows_flattened, axis=1),
        ),
        "head",
    )
    feature_mean = first_sum / feature_total_count
    variance = second_sum / feature_total_count - feature_mean * feature_mean
    inverse_deviation = 1.0 / jnp.sqrt(variance + EPSILON)
    normalized_input = (attended_rows_flattened - feature_mean[:, None]) * inverse_deviation[
        :, None
    ]
    normed = (normalized_input * sublayer_norm_gain[None, :]).astype(jnp.bfloat16)
    normalized_gradient = cotangent.astype(jnp.float32) * sublayer_norm_gain[None, :]
    gradient_sum_first, gradient_sum_second = lax.psum(
        (
            jnp.sum(normalized_gradient, axis=1),
            jnp.sum(normalized_gradient * normalized_input, axis=1),
        ),
        "head",
    )
    attended_gradient = (
        (
            normalized_gradient
            - gradient_sum_first[:, None] / feature_total_count
            - normalized_input * gradient_sum_second[:, None] / feature_total_count
        )
        * inverse_deviation[:, None]
    ).astype(jnp.bfloat16)
    dout_all = attended_gradient.reshape(shape3)
    delta = jnp.sum(dout_all.astype(jnp.float32) * attended.astype(jnp.float32), axis=-1)
    query_acc = jnp.zeros(shape3, jnp.float32)
    key_acc = jnp.zeros(shape3, jnp.float32)
    value_acc = jnp.zeros(shape3, jnp.float32)
    for level_num in range(level_count):
        stride, picked_rows, group_bits, seg_count, mask_table = level_layout(level_num)
        query_sel = pick_rows(query_all, mask_table, stride)
        key_sel = pick_rows(key_all, mask_table, stride)
        value_sel = pick_rows(value_all, mask_table, stride)
        dout_sel = pick_rows(dout_all, mask_table, stride)
        lse_sel = pick_rows(log_total, mask_table, stride)
        delta_sel = pick_rows(delta, mask_table, stride)
        key_group, value_group = stored[level_num]
        query_seg = query_sel.reshape(seg_count, -1, head_local, head_size)
        dout_seg = dout_sel.reshape(seg_count, -1, head_local, head_size)
        lse_seg = lse_sel.reshape(seg_count, -1, head_local)
        delta_seg = delta_sel.reshape(seg_count, -1, head_local)
        key_seg = key_group.reshape(seg_count, SEG0, head_local, head_size)
        value_seg = value_group.reshape(seg_count, SEG0, head_local, head_size)
        query_part, unused_key, unused_value = grad_block(
            query_seg, key_seg, value_seg, dout_seg, lse_seg, delta_seg, score_scale, True, False
        )
        query_group, dout_group = gather_group((query_sel, dout_sel), group_bits)
        lse_group, delta_group = gather_group((lse_sel, delta_sel), group_bits)
        unused_query, key_part, value_part = grad_block(
            query_group.reshape(seg_count, SEG0, head_local, head_size),
            key_sel.reshape(seg_count, -1, head_local, head_size),
            value_sel.reshape(seg_count, -1, head_local, head_size),
            dout_group.reshape(seg_count, SEG0, head_local, head_size),
            lse_group.reshape(seg_count, SEG0, head_local),
            delta_group.reshape(seg_count, SEG0, head_local),
            score_scale,
            False,
            True,
        )
        key_own = key_part.reshape(picked_rows, head_local, head_size)
        value_own = value_part.reshape(picked_rows, head_local, head_size)
        query_acc = query_acc + put_rows(
            query_part.reshape(picked_rows, head_local, head_size), mask_table, stride, 0.0
        )
        key_acc = key_acc + put_rows(key_own, mask_table, stride, 0.0)
        value_acc = value_acc + put_rows(value_own, mask_table, stride, 0.0)
    flat_shape = (tok_rows, head_local * head_size)
    query_grad = query_acc.astype(jnp.bfloat16).reshape(flat_shape)
    key_grad = key_acc.astype(jnp.bfloat16).reshape(flat_shape)
    value_grad = value_acc.astype(jnp.bfloat16).reshape(flat_shape)
    return (normed, query_grad, key_grad, value_grad)


def split_mesh(mesh, tok_rows, level_count):
    ctx_count = mesh.shape["ctx"]
    sizes = sorted({max(1, SEG0 * 2**level_num // tok_rows) for level_num in range(level_count)})
    factors = []
    done = 1
    for size in sizes:
        if size > done:
            factors.append(size // done)
            done = size
    factors.append(ctx_count // done)
    names = tuple(f"c{index}" for index in range(len(factors)))
    shape = tuple(reversed(factors)) + (mesh.shape["head"],)
    sub_mesh = jax.sharding.Mesh(
        mesh.devices.reshape(shape), tuple(reversed(names)) + ("head",)
    )
    level_axes = []
    for level_num in range(level_count):
        size = max(1, SEG0 * 2**level_num // tok_rows)
        count = 0
        span = 1
        while span < size:
            span *= factors[count]
            count += 1
        level_axes.append(tuple(reversed(names[:count])))
    return sub_mesh, tuple(reversed(names)), level_axes


def solution(mesh):
    def run(queries, key_rows, value_rows, offsets, sublayer_norm_gain, cotangent):
        tok_rows = queries.shape[0] // mesh.shape["ctx"]
        sub_mesh, ctx_axes, level_axes = split_mesh(mesh, tok_rows, offsets.shape[0])
        rows = P(ctx_axes, "head")
        in_specs = (rows, rows, rows, P(None, "head"), P("head"), rows)
        out_specs = (rows, rows, rows, rows)
        body = partial(on_device, level_axes=level_axes)
        return jax.shard_map(
            body, mesh=sub_mesh, in_specs=in_specs, out_specs=out_specs, check_vma=False
        )(queries, key_rows, value_rows, offsets, sublayer_norm_gain, cotangent)

    return run
```

```python
from functools import partial, reduce
import math

import jax
import jax.numpy as jnp
from jax import lax
from jax.sharding import PartitionSpec as P

SEG0 = 512


NEG_FILL = -1e30
EPSILON = 1e-05


def pick_rows(source, mask_table, stride):
    count = source.shape[0] // stride
    shaped = source.reshape((count, stride) + source.shape[1:])
    chosen = mask_table.reshape((1, stride, mask_table.shape[1]) + (1,) * (source.ndim - 2))
    return jnp.sum(jnp.where(chosen, shaped, jnp.zeros((), source.dtype)), axis=1)


def put_rows(picked, mask_table, stride, filler):
    chosen = mask_table.reshape((1, stride, mask_table.shape[1]) + (1,) * (picked.ndim - 2))
    spread = jnp.where(chosen, picked[:, None], jnp.asarray(filler, picked.dtype))
    return spread.reshape((picked.shape[0] * stride,) + picked.shape[1:])


def gather_group(members, group_axes):
    if not group_axes:
        return members
    stacked = jnp.stack(members, axis=1)
    whole = lax.all_gather(stacked, group_axes, axis=0, tiled=True)
    return tuple(whole[:, index] for index in range(len(members)))


def split_three(values):
    high = lax.reduce_precision(values, exponent_bits=8, mantissa_bits=7)
    rest = values - high
    middle = lax.reduce_precision(rest, exponent_bits=8, mantissa_bits=7)
    low = rest - middle
    return jnp.stack([high, middle, low], axis=-1).astype(jnp.bfloat16)


def gather_rows(query_sel, dout_sel, lse_sel, delta_sel, group_axes):
    if not group_axes:
        return (query_sel, dout_sel, lse_sel, delta_sel)
    rows = query_sel.shape[0]
    width = query_sel.shape[1] * query_sel.shape[2]
    pieces = split_three(jnp.stack([lse_sel, delta_sel], axis=-1))
    flat = jnp.concatenate(
        [query_sel.reshape(rows, width), dout_sel.reshape(rows, width), pieces.reshape(rows, -1)], axis=1
    )
    whole = lax.all_gather(flat, group_axes, axis=0, tiled=True)
    count = whole.shape[0]
    query_group = whole[:, :width].reshape((count,) + query_sel.shape[1:])
    dout_group = whole[:, width : 2 * width].reshape((count,) + query_sel.shape[1:])
    parts = whole[:, 2 * width :].reshape((count,) + pieces.shape[1:]).astype(jnp.float32)
    stats = parts[..., 0] + parts[..., 1] + parts[..., 2]
    return (query_group, dout_group, stats[..., 0], stats[..., 1])


def grad_block(
    query_seg, key_seg, value_seg, dout_seg, lse_seg, delta_seg, score_scale, want_query, want_keys
):
    lse_t = jnp.transpose(lse_seg, (0, 2, 1))[..., None]
    delta_t = jnp.transpose(delta_seg, (0, 2, 1))[..., None]
    scores = (
        jnp.einsum("sqhd,skhd->shqk", query_seg, key_seg, preferred_element_type=jnp.float32)
        * score_scale
    )
    probs = jnp.exp(scores - lse_t)
    dprobs = jnp.einsum("sqhd,skhd->shqk", dout_seg, value_seg, preferred_element_type=jnp.float32)
    dscores = (probs * (dprobs - delta_t)).astype(jnp.bfloat16)
    query_part = None
    key_part = None
    value_part = None
    if want_query:
        query_part = (
            jnp.einsum("shqk,skhd->sqhd", dscores, key_seg, preferred_element_type=jnp.float32)
            * score_scale
        )
    if want_keys:
        probs_half = probs.astype(jnp.bfloat16)
        key_part = (
            jnp.einsum("shqk,sqhd->skhd", dscores, query_seg, preferred_element_type=jnp.float32)
            * score_scale
        )
        value_part = jnp.einsum(
            "shqk,sqhd->skhd", probs_half, dout_seg, preferred_element_type=jnp.float32
        )
    return (query_part, key_part, value_part)


def on_device(queries, key_rows, value_rows, offsets, sublayer_norm_gain, cotangent, level_axes):
    tok_rows = queries.shape[0]
    head_local = offsets.shape[1]
    head_size = queries.shape[1] // head_local
    level_count = offsets.shape[0]
    feature_total_count = lax.axis_size("head") * queries.shape[1]
    score_scale = 1.0 / math.sqrt(head_size)
    shape3 = (tok_rows, head_local, head_size)
    query_all = queries.reshape(shape3)
    key_all = key_rows.reshape(shape3)
    value_all = value_rows.reshape(shape3)

    def level_layout(level_num):
        stride = 2**level_num
        picked_rows = tok_rows // stride
        group_bits = level_axes[level_num]
        seg_count = max(1, picked_rows // SEG0)
        mask_table = jnp.arange(stride, dtype=jnp.int32)[:, None] == offsets[level_num][None, :]
        return (stride, picked_rows, group_bits, seg_count, mask_table)

    stored = []
    maxima = []
    totals = []
    partials = []
    for level_num in range(level_count):
        stride, picked_rows, group_bits, seg_count, mask_table = level_layout(level_num)
        query_sel = pick_rows(query_all, mask_table, stride)
        key_sel = pick_rows(key_all, mask_table, stride)
        value_sel = pick_rows(value_all, mask_table, stride)
        key_group, value_group = gather_group((key_sel, value_sel), group_bits)
        stored.append((key_group, value_group))
        query_seg = query_sel.reshape(seg_count, -1, head_local, head_size)
        key_seg = key_group.reshape(seg_count, SEG0, head_local, head_size)
        value_seg = value_group.reshape(seg_count, SEG0, head_local, head_size)
        scores = (
            jnp.einsum("sqhd,skhd->shqk", query_seg, key_seg, preferred_element_type=jnp.float32)
            * score_scale
        )
        row_max = jnp.max(scores, axis=-1)
        weights = jnp.exp(scores - row_max[..., None])
        row_total = jnp.sum(weights, axis=-1)
        level_out = jnp.einsum(
            "shqk,skhd->sqhd",
            weights.astype(jnp.bfloat16),
            value_seg,
            preferred_element_type=jnp.float32,
        )
        flat_max = jnp.transpose(row_max, (0, 2, 1)).reshape(picked_rows, head_local)
        flat_total = jnp.transpose(row_total, (0, 2, 1)).reshape(picked_rows, head_local)
        maxima.append(put_rows(flat_max, mask_table, stride, NEG_FILL))
        totals.append(put_rows(flat_total, mask_table, stride, 0.0))
        partials.append(
            put_rows(level_out.reshape(picked_rows, head_local, head_size), mask_table, stride, 0.0)
        )
    top_max = reduce(jnp.maximum, maxima)
    factors = [jnp.exp(each_max - top_max) for each_max in maxima]
    total = factors[0] * totals[0]
    summed = factors[0][..., None] * partials[0]
    for level_num in range(1, level_count):
        total = total + factors[level_num] * totals[level_num]
        summed = summed + factors[level_num][..., None] * partials[level_num]
    attended = (summed / total[..., None]).astype(jnp.bfloat16)
    log_total = top_max + jnp.log(total)
    attended_rows_flattened = attended.reshape(tok_rows, -1).astype(jnp.float32)
    first_sum, second_sum = lax.psum(
        (
            jnp.sum(attended_rows_flattened, axis=1),
            jnp.sum(attended_rows_flattened * attended_rows_flattened, axis=1),
        ),
        "head",
    )
    feature_mean = first_sum / feature_total_count
    variance = second_sum / feature_total_count - feature_mean * feature_mean
    inverse_deviation = 1.0 / jnp.sqrt(variance + EPSILON)
    normalized_input = (attended_rows_flattened - feature_mean[:, None]) * inverse_deviation[
        :, None
    ]
    normed = (normalized_input * sublayer_norm_gain[None, :]).astype(jnp.bfloat16)
    normalized_gradient = cotangent.astype(jnp.float32) * sublayer_norm_gain[None, :]
    gradient_sum_first, gradient_sum_second = lax.psum(
        (
            jnp.sum(normalized_gradient, axis=1),
            jnp.sum(normalized_gradient * normalized_input, axis=1),
        ),
        "head",
    )
    attended_gradient = (
        (
            normalized_gradient
            - gradient_sum_first[:, None] / feature_total_count
            - normalized_input * gradient_sum_second[:, None] / feature_total_count
        )
        * inverse_deviation[:, None]
    ).astype(jnp.bfloat16)
    dout_all = attended_gradient.reshape(shape3)
    delta = jnp.sum(dout_all.astype(jnp.float32) * attended.astype(jnp.float32), axis=-1)
    query_acc = jnp.zeros(shape3, jnp.float32)
    key_acc = jnp.zeros(shape3, jnp.float32)
    value_acc = jnp.zeros(shape3, jnp.float32)
    for level_num in range(level_count):
        stride, picked_rows, group_bits, seg_count, mask_table = level_layout(level_num)
        query_sel = pick_rows(query_all, mask_table, stride)
        key_sel = pick_rows(key_all, mask_table, stride)
        value_sel = pick_rows(value_all, mask_table, stride)
        dout_sel = pick_rows(dout_all, mask_table, stride)
        lse_sel = pick_rows(log_total, mask_table, stride)
        delta_sel = pick_rows(delta, mask_table, stride)
        key_group, value_group = stored[level_num]
        query_seg = query_sel.reshape(seg_count, -1, head_local, head_size)
        dout_seg = dout_sel.reshape(seg_count, -1, head_local, head_size)
        lse_seg = lse_sel.reshape(seg_count, -1, head_local)
        delta_seg = delta_sel.reshape(seg_count, -1, head_local)
        key_seg = key_group.reshape(seg_count, SEG0, head_local, head_size)
        value_seg = value_group.reshape(seg_count, SEG0, head_local, head_size)
        query_part, unused_key, unused_value = grad_block(
            query_seg, key_seg, value_seg, dout_seg, lse_seg, delta_seg, score_scale, True, False
        )
        query_group, dout_group, lse_group, delta_group = gather_rows(
            query_sel, dout_sel, lse_sel, delta_sel, group_bits
        )
        unused_query, key_part, value_part = grad_block(
            query_group.reshape(seg_count, SEG0, head_local, head_size),
            key_sel.reshape(seg_count, -1, head_local, head_size),
            value_sel.reshape(seg_count, -1, head_local, head_size),
            dout_group.reshape(seg_count, SEG0, head_local, head_size),
            lse_group.reshape(seg_count, SEG0, head_local),
            delta_group.reshape(seg_count, SEG0, head_local),
            score_scale,
            False,
            True,
        )
        key_own = key_part.reshape(picked_rows, head_local, head_size)
        value_own = value_part.reshape(picked_rows, head_local, head_size)
        query_acc = query_acc + put_rows(
            query_part.reshape(picked_rows, head_local, head_size), mask_table, stride, 0.0
        )
        key_acc = key_acc + put_rows(key_own, mask_table, stride, 0.0)
        value_acc = value_acc + put_rows(value_own, mask_table, stride, 0.0)
    flat_shape = (tok_rows, head_local * head_size)
    query_grad = query_acc.astype(jnp.bfloat16).reshape(flat_shape)
    key_grad = key_acc.astype(jnp.bfloat16).reshape(flat_shape)
    value_grad = value_acc.astype(jnp.bfloat16).reshape(flat_shape)
    return (normed, query_grad, key_grad, value_grad)


def split_mesh(mesh, tok_rows, level_count):
    ctx_count = mesh.shape["ctx"]
    sizes = sorted({max(1, SEG0 * 2**level_num // tok_rows) for level_num in range(level_count)})
    factors = []
    done = 1
    for size in sizes:
        if size > done:
            factors.append(size // done)
            done = size
    factors.append(ctx_count // done)
    names = tuple(f"c{index}" for index in range(len(factors)))
    shape = tuple(reversed(factors)) + (mesh.shape["head"],)
    sub_mesh = jax.sharding.Mesh(
        mesh.devices.reshape(shape), tuple(reversed(names)) + ("head",)
    )
    level_axes = []
    for level_num in range(level_count):
        size = max(1, SEG0 * 2**level_num // tok_rows)
        count = 0
        span = 1
        while span < size:
            span *= factors[count]
            count += 1
        level_axes.append(tuple(reversed(names[:count])))
    return sub_mesh, tuple(reversed(names)), level_axes


def solution(mesh):
    def run(queries, key_rows, value_rows, offsets, sublayer_norm_gain, cotangent):
        tok_rows = queries.shape[0] // mesh.shape["ctx"]
        sub_mesh, ctx_axes, level_axes = split_mesh(mesh, tok_rows, offsets.shape[0])
        rows = P(ctx_axes, "head")
        in_specs = (rows, rows, rows, P(None, "head"), P("head"), rows)
        out_specs = (rows, rows, rows, rows)
        body = partial(on_device, level_axes=level_axes)
        return jax.shard_map(
            body, mesh=sub_mesh, in_specs=in_specs, out_specs=out_specs, check_vma=False
        )(queries, key_rows, value_rows, offsets, sublayer_norm_gain, cotangent)

    return run
```

```python
from functools import partial, reduce
import math

import jax
import jax.numpy as jnp
from jax import lax
from jax.sharding import PartitionSpec as P

SEG0 = 512


NEG_FILL = -1e30
EPSILON = 1e-05


def pick_rows(source, mask_table, stride):
    count = source.shape[0] // stride
    shaped = source.reshape((count, stride) + source.shape[1:])
    chosen = mask_table.reshape((1, stride, mask_table.shape[1]) + (1,) * (source.ndim - 2))
    return jnp.sum(jnp.where(chosen, shaped, jnp.zeros((), source.dtype)), axis=1)


def put_rows(picked, mask_table, stride, filler):
    chosen = mask_table.reshape((1, stride, mask_table.shape[1]) + (1,) * (picked.ndim - 2))
    spread = jnp.where(chosen, picked[:, None], jnp.asarray(filler, picked.dtype))
    return spread.reshape((picked.shape[0] * stride,) + picked.shape[1:])


def exchange(block, group_axes):
    size = 1
    for name in group_axes:
        size *= lax.axis_size(name)
    parts = [block]
    for step in range(1, size):
        parts.append(lax.ppermute(block, group_axes, [(low, low ^ step) for low in range(size)]))
    return jnp.concatenate(parts, 0)


def collect(block, group_axes, direct):
    if direct:
        return exchange(block, group_axes)
    return lax.all_gather(block, group_axes, axis=0, tiled=True)


def gather_group(members, group_axes, direct):
    if not group_axes:
        return members
    stacked = jnp.stack(members, axis=1)
    whole = collect(stacked, group_axes, direct)
    return tuple(whole[:, index] for index in range(len(members)))


def split_three(values):
    high = lax.reduce_precision(values, exponent_bits=8, mantissa_bits=7)
    rest = values - high
    middle = lax.reduce_precision(rest, exponent_bits=8, mantissa_bits=7)
    low = rest - middle
    return jnp.stack([high, middle, low], axis=-1).astype(jnp.bfloat16)


def gather_rows(query_sel, dout_sel, lse_sel, delta_sel, group_axes, direct):
    if not group_axes:
        return (query_sel, dout_sel, lse_sel, delta_sel)
    rows = query_sel.shape[0]
    width = query_sel.shape[1] * query_sel.shape[2]
    pieces = split_three(jnp.stack([lse_sel, delta_sel], axis=-1))
    flat = jnp.concatenate(
        [query_sel.reshape(rows, width), dout_sel.reshape(rows, width), pieces.reshape(rows, -1)], axis=1
    )
    whole = collect(flat, group_axes, direct)
    count = whole.shape[0]
    query_group = whole[:, :width].reshape((count,) + query_sel.shape[1:])
    dout_group = whole[:, width : 2 * width].reshape((count,) + query_sel.shape[1:])
    parts = whole[:, 2 * width :].reshape((count,) + pieces.shape[1:]).astype(jnp.float32)
    stats = parts[..., 0] + parts[..., 1] + parts[..., 2]
    return (query_group, dout_group, stats[..., 0], stats[..., 1])


def grad_block(
    query_seg, key_seg, value_seg, dout_seg, lse_seg, delta_seg, score_scale, want_query, want_keys
):
    lse_t = jnp.transpose(lse_seg, (0, 2, 1))[..., None]
    delta_t = jnp.transpose(delta_seg, (0, 2, 1))[..., None]
    scores = (
        jnp.einsum("sqhd,skhd->shqk", query_seg, key_seg, preferred_element_type=jnp.float32)
        * score_scale
    )
    probs = jnp.exp(scores - lse_t)
    dprobs = jnp.einsum("sqhd,skhd->shqk", dout_seg, value_seg, preferred_element_type=jnp.float32)
    dscores = (probs * (dprobs - delta_t)).astype(jnp.bfloat16)
    query_part = None
    key_part = None
    value_part = None
    if want_query:
        query_part = (
            jnp.einsum("shqk,skhd->sqhd", dscores, key_seg, preferred_element_type=jnp.float32)
            * score_scale
        )
    if want_keys:
        probs_half = probs.astype(jnp.bfloat16)
        key_part = (
            jnp.einsum("shqk,sqhd->skhd", dscores, query_seg, preferred_element_type=jnp.float32)
            * score_scale
        )
        value_part = jnp.einsum(
            "shqk,sqhd->skhd", probs_half, dout_seg, preferred_element_type=jnp.float32
        )
    return (query_part, key_part, value_part)


def on_device(queries, key_rows, value_rows, offsets, sublayer_norm_gain, cotangent, level_axes):
    tok_rows = queries.shape[0]
    head_local = offsets.shape[1]
    head_size = queries.shape[1] // head_local
    level_count = offsets.shape[0]
    feature_total_count = lax.axis_size("head") * queries.shape[1]
    score_scale = 1.0 / math.sqrt(head_size)
    shape3 = (tok_rows, head_local, head_size)
    query_all = queries.reshape(shape3)
    key_all = key_rows.reshape(shape3)
    value_all = value_rows.reshape(shape3)

    def level_layout(level_num):
        stride = 2**level_num
        picked_rows = tok_rows // stride
        group_bits = level_axes[level_num]
        seg_count = max(1, picked_rows // SEG0)
        mask_table = jnp.arange(stride, dtype=jnp.int32)[:, None] == offsets[level_num][None, :]
        return (stride, picked_rows, group_bits, seg_count, mask_table)

    stored = []
    maxima = []
    totals = []
    partials = []
    for level_num in range(level_count):
        stride, picked_rows, group_bits, seg_count, mask_table = level_layout(level_num)
        query_sel = pick_rows(query_all, mask_table, stride)
        key_sel = pick_rows(key_all, mask_table, stride)
        value_sel = pick_rows(value_all, mask_table, stride)
        key_group, value_group = gather_group((key_sel, value_sel), group_bits, level_num == 0)
        stored.append((key_group, value_group))
        query_seg = query_sel.reshape(seg_count, -1, head_local, head_size)
        key_seg = key_group.reshape(seg_count, SEG0, head_local, head_size)
        value_seg = value_group.reshape(seg_count, SEG0, head_local, head_size)
        scores = (
            jnp.einsum("sqhd,skhd->shqk", query_seg, key_seg, preferred_element_type=jnp.float32)
            * score_scale
        )
        row_max = jnp.max(scores, axis=-1)
        weights = jnp.exp(scores - row_max[..., None])
        row_total = jnp.sum(weights, axis=-1)
        level_out = jnp.einsum(
            "shqk,skhd->sqhd",
            weights.astype(jnp.bfloat16),
            value_seg,
            preferred_element_type=jnp.float32,
        )
        flat_max = jnp.transpose(row_max, (0, 2, 1)).reshape(picked_rows, head_local)
        flat_total = jnp.transpose(row_total, (0, 2, 1)).reshape(picked_rows, head_local)
        maxima.append(put_rows(flat_max, mask_table, stride, NEG_FILL))
        totals.append(put_rows(flat_total, mask_table, stride, 0.0))
        partials.append(
            put_rows(level_out.reshape(picked_rows, head_local, head_size), mask_table, stride, 0.0)
        )
    top_max = reduce(jnp.maximum, maxima)
    factors = [jnp.exp(each_max - top_max) for each_max in maxima]
    total = factors[0] * totals[0]
    summed = factors[0][..., None] * partials[0]
    for level_num in range(1, level_count):
        total = total + factors[level_num] * totals[level_num]
        summed = summed + factors[level_num][..., None] * partials[level_num]
    attended = (summed / total[..., None]).astype(jnp.bfloat16)
    log_total = top_max + jnp.log(total)
    attended_rows_flattened = attended.reshape(tok_rows, -1).astype(jnp.float32)
    first_sum, second_sum = lax.psum(
        (
            jnp.sum(attended_rows_flattened, axis=1),
            jnp.sum(attended_rows_flattened * attended_rows_flattened, axis=1),
        ),
        "head",
    )
    feature_mean = first_sum / feature_total_count
    variance = second_sum / feature_total_count - feature_mean * feature_mean
    inverse_deviation = 1.0 / jnp.sqrt(variance + EPSILON)
    normalized_input = (attended_rows_flattened - feature_mean[:, None]) * inverse_deviation[
        :, None
    ]
    normed = (normalized_input * sublayer_norm_gain[None, :]).astype(jnp.bfloat16)
    normalized_gradient = cotangent.astype(jnp.float32) * sublayer_norm_gain[None, :]
    gradient_sum_first, gradient_sum_second = lax.psum(
        (
            jnp.sum(normalized_gradient, axis=1),
            jnp.sum(normalized_gradient * normalized_input, axis=1),
        ),
        "head",
    )
    attended_gradient = (
        (
            normalized_gradient
            - gradient_sum_first[:, None] / feature_total_count
            - normalized_input * gradient_sum_second[:, None] / feature_total_count
        )
        * inverse_deviation[:, None]
    ).astype(jnp.bfloat16)
    dout_all = attended_gradient.reshape(shape3)
    delta = jnp.sum(dout_all.astype(jnp.float32) * attended.astype(jnp.float32), axis=-1)
    query_acc = jnp.zeros(shape3, jnp.float32)
    key_acc = jnp.zeros(shape3, jnp.float32)
    value_acc = jnp.zeros(shape3, jnp.float32)
    for level_num in range(level_count):
        stride, picked_rows, group_bits, seg_count, mask_table = level_layout(level_num)
        query_sel = pick_rows(query_all, mask_table, stride)
        key_sel = pick_rows(key_all, mask_table, stride)
        value_sel = pick_rows(value_all, mask_table, stride)
        dout_sel = pick_rows(dout_all, mask_table, stride)
        lse_sel = pick_rows(log_total, mask_table, stride)
        delta_sel = pick_rows(delta, mask_table, stride)
        key_group, value_group = stored[level_num]
        query_seg = query_sel.reshape(seg_count, -1, head_local, head_size)
        dout_seg = dout_sel.reshape(seg_count, -1, head_local, head_size)
        lse_seg = lse_sel.reshape(seg_count, -1, head_local)
        delta_seg = delta_sel.reshape(seg_count, -1, head_local)
        key_seg = key_group.reshape(seg_count, SEG0, head_local, head_size)
        value_seg = value_group.reshape(seg_count, SEG0, head_local, head_size)
        query_part, unused_key, unused_value = grad_block(
            query_seg, key_seg, value_seg, dout_seg, lse_seg, delta_seg, score_scale, True, False
        )
        query_group, dout_group, lse_group, delta_group = gather_rows(
            query_sel, dout_sel, lse_sel, delta_sel, group_bits, level_num == 0
        )
        unused_query, key_part, value_part = grad_block(
            query_group.reshape(seg_count, SEG0, head_local, head_size),
            key_sel.reshape(seg_count, -1, head_local, head_size),
            value_sel.reshape(seg_count, -1, head_local, head_size),
            dout_group.reshape(seg_count, SEG0, head_local, head_size),
            lse_group.reshape(seg_count, SEG0, head_local),
            delta_group.reshape(seg_count, SEG0, head_local),
            score_scale,
            False,
            True,
        )
        key_own = key_part.reshape(picked_rows, head_local, head_size)
        value_own = value_part.reshape(picked_rows, head_local, head_size)
        query_acc = query_acc + put_rows(
            query_part.reshape(picked_rows, head_local, head_size), mask_table, stride, 0.0
        )
        key_acc = key_acc + put_rows(key_own, mask_table, stride, 0.0)
        value_acc = value_acc + put_rows(value_own, mask_table, stride, 0.0)
    flat_shape = (tok_rows, head_local * head_size)
    query_grad = query_acc.astype(jnp.bfloat16).reshape(flat_shape)
    key_grad = key_acc.astype(jnp.bfloat16).reshape(flat_shape)
    value_grad = value_acc.astype(jnp.bfloat16).reshape(flat_shape)
    return (normed, query_grad, key_grad, value_grad)


def split_mesh(mesh, tok_rows, level_count):
    ctx_count = mesh.shape["ctx"]
    sizes = sorted({max(1, SEG0 * 2**level_num // tok_rows) for level_num in range(level_count)})
    factors = []
    done = 1
    for size in sizes:
        if size > done:
            factors.append(size // done)
            done = size
    factors.append(ctx_count // done)
    names = tuple(f"c{index}" for index in range(len(factors)))
    shape = tuple(reversed(factors)) + (mesh.shape["head"],)
    sub_mesh = jax.sharding.Mesh(
        mesh.devices.reshape(shape), tuple(reversed(names)) + ("head",)
    )
    level_axes = []
    for level_num in range(level_count):
        size = max(1, SEG0 * 2**level_num // tok_rows)
        count = 0
        span = 1
        while span < size:
            span *= factors[count]
            count += 1
        level_axes.append(tuple(reversed(names[:count])))
    return sub_mesh, tuple(reversed(names)), level_axes


def solution(mesh):
    def run(queries, key_rows, value_rows, offsets, sublayer_norm_gain, cotangent):
        tok_rows = queries.shape[0] // mesh.shape["ctx"]
        sub_mesh, ctx_axes, level_axes = split_mesh(mesh, tok_rows, offsets.shape[0])
        rows = P(ctx_axes, "head")
        in_specs = (rows, rows, rows, P(None, "head"), P("head"), rows)
        out_specs = (rows, rows, rows, rows)
        body = partial(on_device, level_axes=level_axes)
        return jax.shard_map(
            body, mesh=sub_mesh, in_specs=in_specs, out_specs=out_specs, check_vma=False
        )(queries, key_rows, value_rows, offsets, sublayer_norm_gain, cotangent)

    return run
```

```python
from functools import partial, reduce
import math

import jax
import jax.numpy as jnp
from jax import lax
from jax.sharding import PartitionSpec as P

SEG0 = 512


NEG_FILL = -1e30
EPSILON = 1e-05


def pick_rows(source, mask_table, stride):
    count = source.shape[0] // stride
    shaped = source.reshape((count, stride) + source.shape[1:])
    chosen = mask_table.reshape((1, stride, mask_table.shape[1]) + (1,) * (source.ndim - 2))
    return jnp.sum(jnp.where(chosen, shaped, jnp.zeros((), source.dtype)), axis=1)


def put_rows(picked, mask_table, stride, filler):
    chosen = mask_table.reshape((1, stride, mask_table.shape[1]) + (1,) * (picked.ndim - 2))
    spread = jnp.where(chosen, picked[:, None], jnp.asarray(filler, picked.dtype))
    return spread.reshape((picked.shape[0] * stride,) + picked.shape[1:])


def exchange(block, group_axes):
    size = 1
    for name in group_axes:
        size *= lax.axis_size(name)
    parts = [block]
    for step in range(1, size):
        parts.append(lax.ppermute(block, group_axes, [(low, low ^ step) for low in range(size)]))
    return jnp.concatenate(parts, 0)


def collect(block, group_axes, direct):
    if direct:
        return exchange(block, group_axes)
    return lax.all_gather(block, group_axes, axis=0, tiled=True)


def gather_group(members, group_axes, direct):
    if not group_axes:
        return members
    stacked = jnp.stack(members, axis=1)
    whole = collect(stacked, group_axes, direct)
    return tuple(whole[:, index] for index in range(len(members)))


def split_three(values):
    high = lax.reduce_precision(values, exponent_bits=8, mantissa_bits=7)
    rest = values - high
    middle = lax.reduce_precision(rest, exponent_bits=8, mantissa_bits=7)
    low = rest - middle
    return jnp.stack([high, middle, low], axis=-1).astype(jnp.bfloat16)


def gather_rows(dout_sel, lse_sel, delta_sel, group_axes, direct):
    if not group_axes:
        return (dout_sel, lse_sel, delta_sel)
    rows = dout_sel.shape[0]
    width = dout_sel.shape[1] * dout_sel.shape[2]
    pieces = split_three(jnp.stack([lse_sel, delta_sel], axis=-1))
    flat = jnp.concatenate([dout_sel.reshape(rows, width), pieces.reshape(rows, -1)], axis=1)
    whole = collect(flat, group_axes, direct)
    count = whole.shape[0]
    dout_group = whole[:, :width].reshape((count,) + dout_sel.shape[1:])
    parts = whole[:, width:].reshape((count,) + pieces.shape[1:]).astype(jnp.float32)
    stats = parts[..., 0] + parts[..., 1] + parts[..., 2]
    return (dout_group, stats[..., 0], stats[..., 1])


def grad_block(
    query_seg, key_seg, value_seg, dout_seg, lse_seg, delta_seg, score_scale, want_query, want_keys
):
    lse_t = jnp.transpose(lse_seg, (0, 2, 1))[..., None]
    delta_t = jnp.transpose(delta_seg, (0, 2, 1))[..., None]
    scores = (
        jnp.einsum("sqhd,skhd->shqk", query_seg, key_seg, preferred_element_type=jnp.float32)
        * score_scale
    )
    probs = jnp.exp(scores - lse_t)
    dprobs = jnp.einsum("sqhd,skhd->shqk", dout_seg, value_seg, preferred_element_type=jnp.float32)
    dscores = (probs * (dprobs - delta_t)).astype(jnp.bfloat16)
    query_part = None
    key_part = None
    value_part = None
    if want_query:
        query_part = (
            jnp.einsum("shqk,skhd->sqhd", dscores, key_seg, preferred_element_type=jnp.float32)
            * score_scale
        )
    if want_keys:
        probs_half = probs.astype(jnp.bfloat16)
        key_part = (
            jnp.einsum("shqk,sqhd->skhd", dscores, query_seg, preferred_element_type=jnp.float32)
            * score_scale
        )
        value_part = jnp.einsum(
            "shqk,sqhd->skhd", probs_half, dout_seg, preferred_element_type=jnp.float32
        )
    return (query_part, key_part, value_part)


def on_device(queries, key_rows, value_rows, offsets, sublayer_norm_gain, cotangent, level_axes):
    tok_rows = queries.shape[0]
    head_local = offsets.shape[1]
    head_size = queries.shape[1] // head_local
    level_count = offsets.shape[0]
    feature_total_count = lax.axis_size("head") * queries.shape[1]
    score_scale = 1.0 / math.sqrt(head_size)
    shape3 = (tok_rows, head_local, head_size)
    query_all = queries.reshape(shape3)
    key_all = key_rows.reshape(shape3)
    value_all = value_rows.reshape(shape3)

    def level_layout(level_num):
        stride = 2**level_num
        picked_rows = tok_rows // stride
        group_bits = level_axes[level_num]
        seg_count = max(1, picked_rows // SEG0)
        mask_table = jnp.arange(stride, dtype=jnp.int32)[:, None] == offsets[level_num][None, :]
        return (stride, picked_rows, group_bits, seg_count, mask_table)

    stored = []
    maxima = []
    totals = []
    partials = []
    for level_num in range(level_count):
        stride, picked_rows, group_bits, seg_count, mask_table = level_layout(level_num)
        query_sel = pick_rows(query_all, mask_table, stride)
        key_sel = pick_rows(key_all, mask_table, stride)
        value_sel = pick_rows(value_all, mask_table, stride)
        key_group, value_group = gather_group((key_sel, value_sel), group_bits, level_num == 0)
        (query_group,) = gather_group((query_sel,), group_bits, level_num == 0)
        stored.append((key_group, value_group, query_group))
        query_seg = query_sel.reshape(seg_count, -1, head_local, head_size)
        key_seg = key_group.reshape(seg_count, SEG0, head_local, head_size)
        value_seg = value_group.reshape(seg_count, SEG0, head_local, head_size)
        scores = (
            jnp.einsum("sqhd,skhd->shqk", query_seg, key_seg, preferred_element_type=jnp.float32)
            * score_scale
        )
        row_max = jnp.max(scores, axis=-1)
        weights = jnp.exp(scores - row_max[..., None])
        row_total = jnp.sum(weights, axis=-1)
        level_out = jnp.einsum(
            "shqk,skhd->sqhd",
            weights.astype(jnp.bfloat16),
            value_seg,
            preferred_element_type=jnp.float32,
        )
        flat_max = jnp.transpose(row_max, (0, 2, 1)).reshape(picked_rows, head_local)
        flat_total = jnp.transpose(row_total, (0, 2, 1)).reshape(picked_rows, head_local)
        maxima.append(put_rows(flat_max, mask_table, stride, NEG_FILL))
        totals.append(put_rows(flat_total, mask_table, stride, 0.0))
        partials.append(
            put_rows(level_out.reshape(picked_rows, head_local, head_size), mask_table, stride, 0.0)
        )
    top_max = reduce(jnp.maximum, maxima)
    factors = [jnp.exp(each_max - top_max) for each_max in maxima]
    total = factors[0] * totals[0]
    summed = factors[0][..., None] * partials[0]
    for level_num in range(1, level_count):
        total = total + factors[level_num] * totals[level_num]
        summed = summed + factors[level_num][..., None] * partials[level_num]
    attended = (summed / total[..., None]).astype(jnp.bfloat16)
    log_total = top_max + jnp.log(total)
    attended_rows_flattened = attended.reshape(tok_rows, -1).astype(jnp.float32)
    first_sum, second_sum = lax.psum(
        (
            jnp.sum(attended_rows_flattened, axis=1),
            jnp.sum(attended_rows_flattened * attended_rows_flattened, axis=1),
        ),
        "head",
    )
    feature_mean = first_sum / feature_total_count
    variance = second_sum / feature_total_count - feature_mean * feature_mean
    inverse_deviation = 1.0 / jnp.sqrt(variance + EPSILON)
    normalized_input = (attended_rows_flattened - feature_mean[:, None]) * inverse_deviation[
        :, None
    ]
    normed = (normalized_input * sublayer_norm_gain[None, :]).astype(jnp.bfloat16)
    normalized_gradient = cotangent.astype(jnp.float32) * sublayer_norm_gain[None, :]
    gradient_sum_first, gradient_sum_second = lax.psum(
        (
            jnp.sum(normalized_gradient, axis=1),
            jnp.sum(normalized_gradient * normalized_input, axis=1),
        ),
        "head",
    )
    attended_gradient = (
        (
            normalized_gradient
            - gradient_sum_first[:, None] / feature_total_count
            - normalized_input * gradient_sum_second[:, None] / feature_total_count
        )
        * inverse_deviation[:, None]
    ).astype(jnp.bfloat16)
    dout_all = attended_gradient.reshape(shape3)
    delta = jnp.sum(dout_all.astype(jnp.float32) * attended.astype(jnp.float32), axis=-1)
    query_acc = jnp.zeros(shape3, jnp.float32)
    key_acc = jnp.zeros(shape3, jnp.float32)
    value_acc = jnp.zeros(shape3, jnp.float32)
    for level_num in range(level_count):
        stride, picked_rows, group_bits, seg_count, mask_table = level_layout(level_num)
        query_sel = pick_rows(query_all, mask_table, stride)
        key_sel = pick_rows(key_all, mask_table, stride)
        value_sel = pick_rows(value_all, mask_table, stride)
        dout_sel = pick_rows(dout_all, mask_table, stride)
        lse_sel = pick_rows(log_total, mask_table, stride)
        delta_sel = pick_rows(delta, mask_table, stride)
        key_group, value_group, query_group = stored[level_num]
        query_seg = query_sel.reshape(seg_count, -1, head_local, head_size)
        dout_seg = dout_sel.reshape(seg_count, -1, head_local, head_size)
        lse_seg = lse_sel.reshape(seg_count, -1, head_local)
        delta_seg = delta_sel.reshape(seg_count, -1, head_local)
        key_seg = key_group.reshape(seg_count, SEG0, head_local, head_size)
        value_seg = value_group.reshape(seg_count, SEG0, head_local, head_size)
        query_part, unused_key, unused_value = grad_block(
            query_seg, key_seg, value_seg, dout_seg, lse_seg, delta_seg, score_scale, True, False
        )
        dout_group, lse_group, delta_group = gather_rows(
            dout_sel, lse_sel, delta_sel, group_bits, level_num == 0
        )
        unused_query, key_part, value_part = grad_block(
            query_group.reshape(seg_count, SEG0, head_local, head_size),
            key_sel.reshape(seg_count, -1, head_local, head_size),
            value_sel.reshape(seg_count, -1, head_local, head_size),
            dout_group.reshape(seg_count, SEG0, head_local, head_size),
            lse_group.reshape(seg_count, SEG0, head_local),
            delta_group.reshape(seg_count, SEG0, head_local),
            score_scale,
            False,
            True,
        )
        key_own = key_part.reshape(picked_rows, head_local, head_size)
        value_own = value_part.reshape(picked_rows, head_local, head_size)
        query_acc = query_acc + put_rows(
            query_part.reshape(picked_rows, head_local, head_size), mask_table, stride, 0.0
        )
        key_acc = key_acc + put_rows(key_own, mask_table, stride, 0.0)
        value_acc = value_acc + put_rows(value_own, mask_table, stride, 0.0)
    flat_shape = (tok_rows, head_local * head_size)
    query_grad = query_acc.astype(jnp.bfloat16).reshape(flat_shape)
    key_grad = key_acc.astype(jnp.bfloat16).reshape(flat_shape)
    value_grad = value_acc.astype(jnp.bfloat16).reshape(flat_shape)
    return (normed, query_grad, key_grad, value_grad)


def split_mesh(mesh, tok_rows, level_count):
    ctx_count = mesh.shape["ctx"]
    sizes = sorted({max(1, SEG0 * 2**level_num // tok_rows) for level_num in range(level_count)})
    factors = []
    done = 1
    for size in sizes:
        if size > done:
            factors.append(size // done)
            done = size
    factors.append(ctx_count // done)
    names = tuple(f"c{index}" for index in range(len(factors)))
    shape = tuple(reversed(factors)) + (mesh.shape["head"],)
    sub_mesh = jax.sharding.Mesh(
        mesh.devices.reshape(shape), tuple(reversed(names)) + ("head",)
    )
    level_axes = []
    for level_num in range(level_count):
        size = max(1, SEG0 * 2**level_num // tok_rows)
        count = 0
        span = 1
        while span < size:
            span *= factors[count]
            count += 1
        level_axes.append(tuple(reversed(names[:count])))
    return sub_mesh, tuple(reversed(names)), level_axes


def solution(mesh):
    def run(queries, key_rows, value_rows, offsets, sublayer_norm_gain, cotangent):
        tok_rows = queries.shape[0] // mesh.shape["ctx"]
        sub_mesh, ctx_axes, level_axes = split_mesh(mesh, tok_rows, offsets.shape[0])
        rows = P(ctx_axes, "head")
        in_specs = (rows, rows, rows, P(None, "head"), P("head"), rows)
        out_specs = (rows, rows, rows, rows)
        body = partial(on_device, level_axes=level_axes)
        return jax.shard_map(
            body, mesh=sub_mesh, in_specs=in_specs, out_specs=out_specs, check_vma=False
        )(queries, key_rows, value_rows, offsets, sublayer_norm_gain, cotangent)

    return run
```

```python
from functools import partial, reduce
import math

import jax
import jax.numpy as jnp
from jax import lax
from jax.sharding import PartitionSpec as P

SEG0 = 512


NEG_FILL = -1e30
EPSILON = 1e-05


def pick_rows(source, mask_table, stride):
    count = source.shape[0] // stride
    shaped = source.reshape((count, stride) + source.shape[1:])
    chosen = mask_table.reshape((1, stride, mask_table.shape[1]) + (1,) * (source.ndim - 2))
    return jnp.sum(jnp.where(chosen, shaped, jnp.zeros((), source.dtype)), axis=1)


def put_rows(picked, mask_table, stride, filler):
    chosen = mask_table.reshape((1, stride, mask_table.shape[1]) + (1,) * (picked.ndim - 2))
    spread = jnp.where(chosen, picked[:, None], jnp.asarray(filler, picked.dtype))
    return spread.reshape((picked.shape[0] * stride,) + picked.shape[1:])


def exchange(block, group_axes):
    size = 1
    for name in group_axes:
        size *= lax.axis_size(name)
    parts = [block]
    for step in range(1, size):
        parts.append(lax.ppermute(block, group_axes, [(low, low ^ step) for low in range(size)]))
    return jnp.concatenate(parts, 0)


def collect(block, group_axes, direct):
    if direct:
        return exchange(block, group_axes)
    return lax.all_gather(block, group_axes, axis=0, tiled=True)


def gather_group(members, group_axes, direct):
    if not group_axes:
        return members
    stacked = jnp.stack(members, axis=1)
    whole = collect(stacked, group_axes, direct)
    return tuple(whole[:, index] for index in range(len(members)))


def split_three(values):
    high = lax.reduce_precision(values, exponent_bits=8, mantissa_bits=7)
    rest = values - high
    middle = lax.reduce_precision(rest, exponent_bits=8, mantissa_bits=7)
    low = rest - middle
    return jnp.stack([high, middle, low], axis=-1).astype(jnp.bfloat16)


def gather_rows(dout_sel, lse_sel, delta_sel, group_axes, direct):
    if not group_axes:
        return (dout_sel, lse_sel, delta_sel)
    rows = dout_sel.shape[0]
    width = dout_sel.shape[1] * dout_sel.shape[2]
    pieces = split_three(jnp.stack([lse_sel, delta_sel], axis=-1))
    flat = jnp.concatenate([dout_sel.reshape(rows, width), pieces.reshape(rows, -1)], axis=1)
    whole = collect(flat, group_axes, direct)
    count = whole.shape[0]
    dout_group = whole[:, :width].reshape((count,) + dout_sel.shape[1:])
    parts = whole[:, width:].reshape((count,) + pieces.shape[1:]).astype(jnp.float32)
    stats = parts[..., 0] + parts[..., 1] + parts[..., 2]
    return (dout_group, stats[..., 0], stats[..., 1])


def grad_block(
    query_seg, key_seg, value_seg, dout_seg, lse_seg, delta_seg, score_scale, want_query, want_keys
):
    lse_t = jnp.transpose(lse_seg, (0, 2, 1))[..., None]
    delta_t = jnp.transpose(delta_seg, (0, 2, 1))[..., None]
    scores = (
        jnp.einsum("sqhd,skhd->shqk", query_seg, key_seg, preferred_element_type=jnp.float32)
        * score_scale
    )
    probs = jnp.exp(scores - lse_t)
    dprobs = jnp.einsum("sqhd,skhd->shqk", dout_seg, value_seg, preferred_element_type=jnp.float32)
    dscores = (probs * (dprobs - delta_t)).astype(jnp.bfloat16)
    query_part = None
    key_part = None
    value_part = None
    if want_query:
        query_part = (
            jnp.einsum("shqk,skhd->sqhd", dscores, key_seg, preferred_element_type=jnp.float32)
            * score_scale
        )
    if want_keys:
        probs_half = probs.astype(jnp.bfloat16)
        key_part = (
            jnp.einsum("shqk,sqhd->skhd", dscores, query_seg, preferred_element_type=jnp.float32)
            * score_scale
        )
        value_part = jnp.einsum(
            "shqk,sqhd->skhd", probs_half, dout_seg, preferred_element_type=jnp.float32
        )
    return (query_part, key_part, value_part)


def on_device(queries, key_rows, value_rows, offsets, sublayer_norm_gain, cotangent, level_axes):
    tok_rows = queries.shape[0]
    head_local = offsets.shape[1]
    head_size = queries.shape[1] // head_local
    level_count = offsets.shape[0]
    feature_total_count = lax.axis_size("head") * queries.shape[1]
    score_scale = 1.0 / math.sqrt(head_size)
    shape3 = (tok_rows, head_local, head_size)
    query_all = queries.reshape(shape3)
    key_all = key_rows.reshape(shape3)
    value_all = value_rows.reshape(shape3)

    def level_layout(level_num):
        stride = 2**level_num
        picked_rows = tok_rows // stride
        group_bits = level_axes[level_num]
        seg_count = max(1, picked_rows // SEG0)
        mask_table = jnp.arange(stride, dtype=jnp.int32)[:, None] == offsets[level_num][None, :]
        return (stride, picked_rows, group_bits, seg_count, mask_table)

    stored = []
    maxima = []
    totals = []
    partials = []
    for level_num in range(level_count):
        stride, picked_rows, group_bits, seg_count, mask_table = level_layout(level_num)
        query_sel = pick_rows(query_all, mask_table, stride)
        key_sel = pick_rows(key_all, mask_table, stride)
        value_sel = pick_rows(value_all, mask_table, stride)
        key_group, value_group, query_group = gather_group(
            (key_sel, value_sel, query_sel), group_bits, level_num == 0
        )
        stored.append((key_group, value_group, query_group))
        query_seg = query_sel.reshape(seg_count, -1, head_local, head_size)
        key_seg = key_group.reshape(seg_count, SEG0, head_local, head_size)
        value_seg = value_group.reshape(seg_count, SEG0, head_local, head_size)
        scores = (
            jnp.einsum("sqhd,skhd->shqk", query_seg, key_seg, preferred_element_type=jnp.float32)
            * score_scale
        )
        row_max = jnp.max(scores, axis=-1)
        weights = jnp.exp(scores - row_max[..., None])
        row_total = jnp.sum(weights, axis=-1)
        level_out = jnp.einsum(
            "shqk,skhd->sqhd",
            weights.astype(jnp.bfloat16),
            value_seg,
            preferred_element_type=jnp.float32,
        )
        flat_max = jnp.transpose(row_max, (0, 2, 1)).reshape(picked_rows, head_local)
        flat_total = jnp.transpose(row_total, (0, 2, 1)).reshape(picked_rows, head_local)
        maxima.append(put_rows(flat_max, mask_table, stride, NEG_FILL))
        totals.append(put_rows(flat_total, mask_table, stride, 0.0))
        partials.append(
            put_rows(level_out.reshape(picked_rows, head_local, head_size), mask_table, stride, 0.0)
        )
    top_max = reduce(jnp.maximum, maxima)
    factors = [jnp.exp(each_max - top_max) for each_max in maxima]
    total = factors[0] * totals[0]
    summed = factors[0][..., None] * partials[0]
    for level_num in range(1, level_count):
        total = total + factors[level_num] * totals[level_num]
        summed = summed + factors[level_num][..., None] * partials[level_num]
    attended = (summed / total[..., None]).astype(jnp.bfloat16)
    log_total = top_max + jnp.log(total)
    attended_rows_flattened = attended.reshape(tok_rows, -1).astype(jnp.float32)
    first_sum, second_sum = lax.psum(
        (
            jnp.sum(attended_rows_flattened, axis=1),
            jnp.sum(attended_rows_flattened * attended_rows_flattened, axis=1),
        ),
        "head",
    )
    feature_mean = first_sum / feature_total_count
    variance = second_sum / feature_total_count - feature_mean * feature_mean
    inverse_deviation = 1.0 / jnp.sqrt(variance + EPSILON)
    normalized_input = (attended_rows_flattened - feature_mean[:, None]) * inverse_deviation[
        :, None
    ]
    normed = (normalized_input * sublayer_norm_gain[None, :]).astype(jnp.bfloat16)
    normalized_gradient = cotangent.astype(jnp.float32) * sublayer_norm_gain[None, :]
    gradient_sum_first, gradient_sum_second = lax.psum(
        (
            jnp.sum(normalized_gradient, axis=1),
            jnp.sum(normalized_gradient * normalized_input, axis=1),
        ),
        "head",
    )
    attended_gradient = (
        (
            normalized_gradient
            - gradient_sum_first[:, None] / feature_total_count
            - normalized_input * gradient_sum_second[:, None] / feature_total_count
        )
        * inverse_deviation[:, None]
    ).astype(jnp.bfloat16)
    dout_all = attended_gradient.reshape(shape3)
    delta = jnp.sum(dout_all.astype(jnp.float32) * attended.astype(jnp.float32), axis=-1)
    query_acc = jnp.zeros(shape3, jnp.float32)
    key_acc = jnp.zeros(shape3, jnp.float32)
    value_acc = jnp.zeros(shape3, jnp.float32)
    for level_num in range(level_count):
        stride, picked_rows, group_bits, seg_count, mask_table = level_layout(level_num)
        query_sel = pick_rows(query_all, mask_table, stride)
        key_sel = pick_rows(key_all, mask_table, stride)
        value_sel = pick_rows(value_all, mask_table, stride)
        dout_sel = pick_rows(dout_all, mask_table, stride)
        lse_sel = pick_rows(log_total, mask_table, stride)
        delta_sel = pick_rows(delta, mask_table, stride)
        key_group, value_group, query_group = stored[level_num]
        query_seg = query_sel.reshape(seg_count, -1, head_local, head_size)
        dout_seg = dout_sel.reshape(seg_count, -1, head_local, head_size)
        lse_seg = lse_sel.reshape(seg_count, -1, head_local)
        delta_seg = delta_sel.reshape(seg_count, -1, head_local)
        key_seg = key_group.reshape(seg_count, SEG0, head_local, head_size)
        value_seg = value_group.reshape(seg_count, SEG0, head_local, head_size)
        query_part, unused_key, unused_value = grad_block(
            query_seg, key_seg, value_seg, dout_seg, lse_seg, delta_seg, score_scale, True, False
        )
        dout_group, lse_group, delta_group = gather_rows(
            dout_sel, lse_sel, delta_sel, group_bits, level_num == 0
        )
        unused_query, key_part, value_part = grad_block(
            query_group.reshape(seg_count, SEG0, head_local, head_size),
            key_sel.reshape(seg_count, -1, head_local, head_size),
            value_sel.reshape(seg_count, -1, head_local, head_size),
            dout_group.reshape(seg_count, SEG0, head_local, head_size),
            lse_group.reshape(seg_count, SEG0, head_local),
            delta_group.reshape(seg_count, SEG0, head_local),
            score_scale,
            False,
            True,
        )
        key_own = key_part.reshape(picked_rows, head_local, head_size)
        value_own = value_part.reshape(picked_rows, head_local, head_size)
        query_acc = query_acc + put_rows(
            query_part.reshape(picked_rows, head_local, head_size), mask_table, stride, 0.0
        )
        key_acc = key_acc + put_rows(key_own, mask_table, stride, 0.0)
        value_acc = value_acc + put_rows(value_own, mask_table, stride, 0.0)
    flat_shape = (tok_rows, head_local * head_size)
    query_grad = query_acc.astype(jnp.bfloat16).reshape(flat_shape)
    key_grad = key_acc.astype(jnp.bfloat16).reshape(flat_shape)
    value_grad = value_acc.astype(jnp.bfloat16).reshape(flat_shape)
    return (normed, query_grad, key_grad, value_grad)


def split_mesh(mesh, tok_rows, level_count):
    ctx_count = mesh.shape["ctx"]
    sizes = sorted({max(1, SEG0 * 2**level_num // tok_rows) for level_num in range(level_count)})
    factors = []
    done = 1
    for size in sizes:
        if size > done:
            factors.append(size // done)
            done = size
    factors.append(ctx_count // done)
    names = tuple(f"c{index}" for index in range(len(factors)))
    shape = tuple(reversed(factors)) + (mesh.shape["head"],)
    sub_mesh = jax.sharding.Mesh(
        mesh.devices.reshape(shape), tuple(reversed(names)) + ("head",)
    )
    level_axes = []
    for level_num in range(level_count):
        size = max(1, SEG0 * 2**level_num // tok_rows)
        count = 0
        span = 1
        while span < size:
            span *= factors[count]
            count += 1
        level_axes.append(tuple(reversed(names[:count])))
    return sub_mesh, tuple(reversed(names)), level_axes


def solution(mesh):
    def run(queries, key_rows, value_rows, offsets, sublayer_norm_gain, cotangent):
        tok_rows = queries.shape[0] // mesh.shape["ctx"]
        sub_mesh, ctx_axes, level_axes = split_mesh(mesh, tok_rows, offsets.shape[0])
        rows = P(ctx_axes, "head")
        in_specs = (rows, rows, rows, P(None, "head"), P("head"), rows)
        out_specs = (rows, rows, rows, rows)
        body = partial(on_device, level_axes=level_axes)
        return jax.shard_map(
            body, mesh=sub_mesh, in_specs=in_specs, out_specs=out_specs, check_vma=False
        )(queries, key_rows, value_rows, offsets, sublayer_norm_gain, cotangent)

    return run
```

```python
from functools import partial, reduce
import math

import jax
import jax.numpy as jnp
from jax import lax
from jax.sharding import PartitionSpec as P

SEG0 = 512


NEG_FILL = -1e30
EPSILON = 1e-05


def pick_rows(source, mask_table, stride):
    count = source.shape[0] // stride
    shaped = source.reshape((count, stride) + source.shape[1:])
    chosen = mask_table.reshape((1, stride, mask_table.shape[1]) + (1,) * (source.ndim - 2))
    return jnp.sum(jnp.where(chosen, shaped, jnp.zeros((), source.dtype)), axis=1)


def put_rows(picked, mask_table, stride, filler):
    chosen = mask_table.reshape((1, stride, mask_table.shape[1]) + (1,) * (picked.ndim - 2))
    spread = jnp.where(chosen, picked[:, None], jnp.asarray(filler, picked.dtype))
    return spread.reshape((picked.shape[0] * stride,) + picked.shape[1:])


def exchange(block, group_axes):
    size = 1
    for name in group_axes:
        size *= lax.axis_size(name)
    parts = [block]
    for step in range(1, size):
        parts.append(lax.ppermute(block, group_axes, [(low, low ^ step) for low in range(size)]))
    return jnp.concatenate(parts, 0)


def collect(block, group_axes, direct):
    if direct:
        return exchange(block, group_axes)
    return lax.all_gather(block, group_axes, axis=0, tiled=True)


def gather_group(members, group_axes, direct):
    if not group_axes:
        return members
    stacked = jnp.stack(members, axis=1)
    whole = collect(stacked, group_axes, direct)
    return tuple(whole[:, index] for index in range(len(members)))


def split_three(values):
    high = lax.reduce_precision(values, exponent_bits=8, mantissa_bits=7)
    rest = values - high
    middle = lax.reduce_precision(rest, exponent_bits=8, mantissa_bits=7)
    low = rest - middle
    return jnp.stack([high, middle, low], axis=-1).astype(jnp.bfloat16)


def gather_rows(members, lse_sel, delta_sel, group_axes, direct):
    if not group_axes:
        return members + (lse_sel, delta_sel)
    rows = lse_sel.shape[0]
    width = members[0].shape[1] * members[0].shape[2]
    pieces = split_three(jnp.stack([lse_sel, delta_sel], axis=-1))
    flat = jnp.concatenate(
        [member.reshape(rows, width) for member in members] + [pieces.reshape(rows, -1)], axis=1
    )
    whole = collect(flat, group_axes, direct)
    count = whole.shape[0]
    groups = tuple(
        whole[:, index * width : (index + 1) * width].reshape((count,) + members[0].shape[1:])
        for index in range(len(members))
    )
    parts = whole[:, len(members) * width :].reshape((count,) + pieces.shape[1:]).astype(jnp.float32)
    stats = parts[..., 0] + parts[..., 1] + parts[..., 2]
    return groups + (stats[..., 0], stats[..., 1])


def grad_block(
    query_seg, key_seg, value_seg, dout_seg, lse_seg, delta_seg, score_scale, want_query, want_keys
):
    lse_t = jnp.transpose(lse_seg, (0, 2, 1))[..., None]
    delta_t = jnp.transpose(delta_seg, (0, 2, 1))[..., None]
    scores = (
        jnp.einsum("sqhd,skhd->shqk", query_seg, key_seg, preferred_element_type=jnp.float32)
        * score_scale
    )
    probs = jnp.exp(scores - lse_t)
    dprobs = jnp.einsum("sqhd,skhd->shqk", dout_seg, value_seg, preferred_element_type=jnp.float32)
    dscores = (probs * (dprobs - delta_t)).astype(jnp.bfloat16)
    query_part = None
    key_part = None
    value_part = None
    if want_query:
        query_part = (
            jnp.einsum("shqk,skhd->sqhd", dscores, key_seg, preferred_element_type=jnp.float32)
            * score_scale
        )
    if want_keys:
        probs_half = probs.astype(jnp.bfloat16)
        key_part = (
            jnp.einsum("shqk,sqhd->skhd", dscores, query_seg, preferred_element_type=jnp.float32)
            * score_scale
        )
        value_part = jnp.einsum(
            "shqk,sqhd->skhd", probs_half, dout_seg, preferred_element_type=jnp.float32
        )
    return (query_part, key_part, value_part)


def on_device(queries, key_rows, value_rows, offsets, sublayer_norm_gain, cotangent, level_axes):
    tok_rows = queries.shape[0]
    head_local = offsets.shape[1]
    head_size = queries.shape[1] // head_local
    level_count = offsets.shape[0]
    feature_total_count = lax.axis_size("head") * queries.shape[1]
    score_scale = 1.0 / math.sqrt(head_size)
    shape3 = (tok_rows, head_local, head_size)
    query_all = queries.reshape(shape3)
    key_all = key_rows.reshape(shape3)
    value_all = value_rows.reshape(shape3)

    def level_layout(level_num):
        stride = 2**level_num
        picked_rows = tok_rows // stride
        group_bits = level_axes[level_num]
        seg_count = max(1, picked_rows // SEG0)
        mask_table = jnp.arange(stride, dtype=jnp.int32)[:, None] == offsets[level_num][None, :]
        return (stride, picked_rows, group_bits, seg_count, mask_table)

    stored = []
    maxima = []
    totals = []
    partials = []
    for level_num in range(level_count):
        stride, picked_rows, group_bits, seg_count, mask_table = level_layout(level_num)
        query_sel = pick_rows(query_all, mask_table, stride)
        key_sel = pick_rows(key_all, mask_table, stride)
        value_sel = pick_rows(value_all, mask_table, stride)
        if level_num == 1:
            key_group, value_group, query_group = gather_group(
                (key_sel, value_sel, query_sel), group_bits, False
            )
        else:
            key_group, value_group = gather_group((key_sel, value_sel), group_bits, level_num == 0)
            query_group = None
        stored.append((key_group, value_group, query_group))
        query_seg = query_sel.reshape(seg_count, -1, head_local, head_size)
        key_seg = key_group.reshape(seg_count, SEG0, head_local, head_size)
        value_seg = value_group.reshape(seg_count, SEG0, head_local, head_size)
        scores = (
            jnp.einsum("sqhd,skhd->shqk", query_seg, key_seg, preferred_element_type=jnp.float32)
            * score_scale
        )
        row_max = jnp.max(scores, axis=-1)
        weights = jnp.exp(scores - row_max[..., None])
        row_total = jnp.sum(weights, axis=-1)
        level_out = jnp.einsum(
            "shqk,skhd->sqhd",
            weights.astype(jnp.bfloat16),
            value_seg,
            preferred_element_type=jnp.float32,
        )
        flat_max = jnp.transpose(row_max, (0, 2, 1)).reshape(picked_rows, head_local)
        flat_total = jnp.transpose(row_total, (0, 2, 1)).reshape(picked_rows, head_local)
        maxima.append(put_rows(flat_max, mask_table, stride, NEG_FILL))
        totals.append(put_rows(flat_total, mask_table, stride, 0.0))
        partials.append(
            put_rows(level_out.reshape(picked_rows, head_local, head_size), mask_table, stride, 0.0)
        )
    top_max = reduce(jnp.maximum, maxima)
    factors = [jnp.exp(each_max - top_max) for each_max in maxima]
    total = factors[0] * totals[0]
    summed = factors[0][..., None] * partials[0]
    for level_num in range(1, level_count):
        total = total + factors[level_num] * totals[level_num]
        summed = summed + factors[level_num][..., None] * partials[level_num]
    attended = (summed / total[..., None]).astype(jnp.bfloat16)
    log_total = top_max + jnp.log(total)
    attended_rows_flattened = attended.reshape(tok_rows, -1).astype(jnp.float32)
    first_sum, second_sum = lax.psum(
        (
            jnp.sum(attended_rows_flattened, axis=1),
            jnp.sum(attended_rows_flattened * attended_rows_flattened, axis=1),
        ),
        "head",
    )
    feature_mean = first_sum / feature_total_count
    variance = second_sum / feature_total_count - feature_mean * feature_mean
    inverse_deviation = 1.0 / jnp.sqrt(variance + EPSILON)
    normalized_input = (attended_rows_flattened - feature_mean[:, None]) * inverse_deviation[
        :, None
    ]
    normed = (normalized_input * sublayer_norm_gain[None, :]).astype(jnp.bfloat16)
    normalized_gradient = cotangent.astype(jnp.float32) * sublayer_norm_gain[None, :]
    gradient_sum_first, gradient_sum_second = lax.psum(
        (
            jnp.sum(normalized_gradient, axis=1),
            jnp.sum(normalized_gradient * normalized_input, axis=1),
        ),
        "head",
    )
    attended_gradient = (
        (
            normalized_gradient
            - gradient_sum_first[:, None] / feature_total_count
            - normalized_input * gradient_sum_second[:, None] / feature_total_count
        )
        * inverse_deviation[:, None]
    ).astype(jnp.bfloat16)
    dout_all = attended_gradient.reshape(shape3)
    delta = jnp.sum(dout_all.astype(jnp.float32) * attended.astype(jnp.float32), axis=-1)
    query_acc = jnp.zeros(shape3, jnp.float32)
    key_acc = jnp.zeros(shape3, jnp.float32)
    value_acc = jnp.zeros(shape3, jnp.float32)
    for level_num in range(level_count):
        stride, picked_rows, group_bits, seg_count, mask_table = level_layout(level_num)
        query_sel = pick_rows(query_all, mask_table, stride)
        key_sel = pick_rows(key_all, mask_table, stride)
        value_sel = pick_rows(value_all, mask_table, stride)
        dout_sel = pick_rows(dout_all, mask_table, stride)
        lse_sel = pick_rows(log_total, mask_table, stride)
        delta_sel = pick_rows(delta, mask_table, stride)
        key_group, value_group, query_group = stored[level_num]
        query_seg = query_sel.reshape(seg_count, -1, head_local, head_size)
        dout_seg = dout_sel.reshape(seg_count, -1, head_local, head_size)
        lse_seg = lse_sel.reshape(seg_count, -1, head_local)
        delta_seg = delta_sel.reshape(seg_count, -1, head_local)
        key_seg = key_group.reshape(seg_count, SEG0, head_local, head_size)
        value_seg = value_group.reshape(seg_count, SEG0, head_local, head_size)
        query_part, unused_key, unused_value = grad_block(
            query_seg, key_seg, value_seg, dout_seg, lse_seg, delta_seg, score_scale, True, False
        )
        if query_group is None:
            query_group, dout_group, lse_group, delta_group = gather_rows(
                (query_sel, dout_sel), lse_sel, delta_sel, group_bits, level_num == 0
            )
        else:
            dout_group, lse_group, delta_group = gather_rows(
                (dout_sel,), lse_sel, delta_sel, group_bits, level_num == 0
            )
        unused_query, key_part, value_part = grad_block(
            query_group.reshape(seg_count, SEG0, head_local, head_size),
            key_sel.reshape(seg_count, -1, head_local, head_size),
            value_sel.reshape(seg_count, -1, head_local, head_size),
            dout_group.reshape(seg_count, SEG0, head_local, head_size),
            lse_group.reshape(seg_count, SEG0, head_local),
            delta_group.reshape(seg_count, SEG0, head_local),
            score_scale,
            False,
            True,
        )
        key_own = key_part.reshape(picked_rows, head_local, head_size)
        value_own = value_part.reshape(picked_rows, head_local, head_size)
        query_acc = query_acc + put_rows(
            query_part.reshape(picked_rows, head_local, head_size), mask_table, stride, 0.0
        )
        key_acc = key_acc + put_rows(key_own, mask_table, stride, 0.0)
        value_acc = value_acc + put_rows(value_own, mask_table, stride, 0.0)
    flat_shape = (tok_rows, head_local * head_size)
    query_grad = query_acc.astype(jnp.bfloat16).reshape(flat_shape)
    key_grad = key_acc.astype(jnp.bfloat16).reshape(flat_shape)
    value_grad = value_acc.astype(jnp.bfloat16).reshape(flat_shape)
    return (normed, query_grad, key_grad, value_grad)


def split_mesh(mesh, tok_rows, level_count):
    ctx_count = mesh.shape["ctx"]
    sizes = sorted({max(1, SEG0 * 2**level_num // tok_rows) for level_num in range(level_count)})
    factors = []
    done = 1
    for size in sizes:
        if size > done:
            factors.append(size // done)
            done = size
    factors.append(ctx_count // done)
    names = tuple(f"c{index}" for index in range(len(factors)))
    shape = tuple(reversed(factors)) + (mesh.shape["head"],)
    sub_mesh = jax.sharding.Mesh(
        mesh.devices.reshape(shape), tuple(reversed(names)) + ("head",)
    )
    level_axes = []
    for level_num in range(level_count):
        size = max(1, SEG0 * 2**level_num // tok_rows)
        count = 0
        span = 1
        while span < size:
            span *= factors[count]
            count += 1
        level_axes.append(tuple(reversed(names[:count])))
    return sub_mesh, tuple(reversed(names)), level_axes


def solution(mesh):
    def run(queries, key_rows, value_rows, offsets, sublayer_norm_gain, cotangent):
        tok_rows = queries.shape[0] // mesh.shape["ctx"]
        sub_mesh, ctx_axes, level_axes = split_mesh(mesh, tok_rows, offsets.shape[0])
        rows = P(ctx_axes, "head")
        in_specs = (rows, rows, rows, P(None, "head"), P("head"), rows)
        out_specs = (rows, rows, rows, rows)
        body = partial(on_device, level_axes=level_axes)
        return jax.shard_map(
            body, mesh=sub_mesh, in_specs=in_specs, out_specs=out_specs, check_vma=False
        )(queries, key_rows, value_rows, offsets, sublayer_norm_gain, cotangent)

    return run
```

```python
from functools import partial, reduce
import math

import jax
import jax.numpy as jnp
from jax import lax
from jax.sharding import PartitionSpec as P

SEG0 = 512


NEG_FILL = -1e30
EPSILON = 1e-05


def pick_rows(source, mask_table, stride):
    count = source.shape[0] // stride
    shaped = source.reshape((count, stride) + source.shape[1:])
    chosen = mask_table.reshape((1, stride, mask_table.shape[1]) + (1,) * (source.ndim - 2))
    return jnp.sum(jnp.where(chosen, shaped, jnp.zeros((), source.dtype)), axis=1)


def put_rows(picked, mask_table, stride, filler):
    chosen = mask_table.reshape((1, stride, mask_table.shape[1]) + (1,) * (picked.ndim - 2))
    spread = jnp.where(chosen, picked[:, None], jnp.asarray(filler, picked.dtype))
    return spread.reshape((picked.shape[0] * stride,) + picked.shape[1:])


def exchange(block, group_axes):
    size = 1
    for name in group_axes:
        size *= lax.axis_size(name)
    parts = [block]
    for step in range(1, size):
        parts.append(lax.ppermute(block, group_axes, [(low, low ^ step) for low in range(size)]))
    return jnp.concatenate(parts, 0)


def collect(block, group_axes, direct):
    if direct:
        return exchange(block, group_axes)
    return lax.all_gather(block, group_axes, axis=0, tiled=True)


def gather_group(members, group_axes, direct):
    if not group_axes:
        return members
    stacked = jnp.stack(members, axis=1)
    whole = collect(stacked, group_axes, direct)
    return tuple(whole[:, index] for index in range(len(members)))


def split_three(values):
    high = lax.reduce_precision(values, exponent_bits=8, mantissa_bits=7)
    rest = values - high
    middle = lax.reduce_precision(rest, exponent_bits=8, mantissa_bits=7)
    low = rest - middle
    return jnp.stack([high, middle, low], axis=-1).astype(jnp.bfloat16)


def gather_rows(dout_sel, lse_sel, delta_sel, group_axes, direct):
    if not group_axes:
        return (dout_sel, lse_sel, delta_sel)
    rows = dout_sel.shape[0]
    width = dout_sel.shape[1] * dout_sel.shape[2]
    pieces = split_three(jnp.stack([lse_sel, delta_sel], axis=-1))
    flat = jnp.concatenate([dout_sel.reshape(rows, width), pieces.reshape(rows, -1)], axis=1)
    whole = collect(flat, group_axes, direct)
    count = whole.shape[0]
    dout_group = whole[:, :width].reshape((count,) + dout_sel.shape[1:])
    parts = whole[:, width:].reshape((count,) + pieces.shape[1:]).astype(jnp.float32)
    stats = parts[..., 0] + parts[..., 1] + parts[..., 2]
    return (dout_group, stats[..., 0], stats[..., 1])


def grad_block(
    query_seg, key_seg, value_seg, dout_seg, lse_seg, delta_seg, score_scale, want_query, want_keys
):
    lse_t = jnp.transpose(lse_seg, (0, 2, 1))[..., None]
    delta_t = jnp.transpose(delta_seg, (0, 2, 1))[..., None]
    scores = (
        jnp.einsum("sqhd,skhd->shqk", query_seg, key_seg, preferred_element_type=jnp.float32)
        * score_scale
    )
    probs = jnp.exp(scores - lse_t)
    dprobs = jnp.einsum("sqhd,skhd->shqk", dout_seg, value_seg, preferred_element_type=jnp.float32)
    dscores = (probs * (dprobs - delta_t)).astype(jnp.bfloat16)
    query_part = None
    key_part = None
    value_part = None
    if want_query:
        query_part = (
            jnp.einsum("shqk,skhd->sqhd", dscores, key_seg, preferred_element_type=jnp.float32)
            * score_scale
        )
    if want_keys:
        probs_half = probs.astype(jnp.bfloat16)
        key_part = (
            jnp.einsum("shqk,sqhd->skhd", dscores, query_seg, preferred_element_type=jnp.float32)
            * score_scale
        )
        value_part = jnp.einsum(
            "shqk,sqhd->skhd", probs_half, dout_seg, preferred_element_type=jnp.float32
        )
    return (query_part, key_part, value_part)


def on_device(queries, key_rows, value_rows, offsets, sublayer_norm_gain, cotangent, level_axes):
    tok_rows = queries.shape[0]
    head_local = offsets.shape[1]
    head_size = queries.shape[1] // head_local
    level_count = offsets.shape[0]
    feature_total_count = lax.axis_size("head") * queries.shape[1]
    score_scale = 1.0 / math.sqrt(head_size)
    shape3 = (tok_rows, head_local, head_size)
    query_all = queries.reshape(shape3)
    key_all = key_rows.reshape(shape3)
    value_all = value_rows.reshape(shape3)

    def level_layout(level_num):
        stride = 2**level_num
        picked_rows = tok_rows // stride
        group_bits = level_axes[level_num]
        seg_count = max(1, picked_rows // SEG0)
        mask_table = jnp.arange(stride, dtype=jnp.int32)[:, None] == offsets[level_num][None, :]
        return (stride, picked_rows, group_bits, seg_count, mask_table)

    stored = []
    maxima = []
    totals = []
    partials = []
    for level_num in range(level_count):
        stride, picked_rows, group_bits, seg_count, mask_table = level_layout(level_num)
        query_sel = pick_rows(query_all, mask_table, stride)
        key_sel = pick_rows(key_all, mask_table, stride)
        value_sel = pick_rows(value_all, mask_table, stride)
        if level_num == 2:
            key_group, value_group = gather_group((key_sel, value_sel), group_bits, False)
            (query_group,) = gather_group((query_sel,), group_bits, False)
        else:
            key_group, value_group, query_group = gather_group(
                (key_sel, value_sel, query_sel), group_bits, level_num == 0
            )
        stored.append((key_group, value_group, query_group))
        query_seg = query_sel.reshape(seg_count, -1, head_local, head_size)
        key_seg = key_group.reshape(seg_count, SEG0, head_local, head_size)
        value_seg = value_group.reshape(seg_count, SEG0, head_local, head_size)
        scores = (
            jnp.einsum("sqhd,skhd->shqk", query_seg, key_seg, preferred_element_type=jnp.float32)
            * score_scale
        )
        row_max = jnp.max(scores, axis=-1)
        weights = jnp.exp(scores - row_max[..., None])
        row_total = jnp.sum(weights, axis=-1)
        level_out = jnp.einsum(
            "shqk,skhd->sqhd",
            weights.astype(jnp.bfloat16),
            value_seg,
            preferred_element_type=jnp.float32,
        )
        flat_max = jnp.transpose(row_max, (0, 2, 1)).reshape(picked_rows, head_local)
        flat_total = jnp.transpose(row_total, (0, 2, 1)).reshape(picked_rows, head_local)
        maxima.append(put_rows(flat_max, mask_table, stride, NEG_FILL))
        totals.append(put_rows(flat_total, mask_table, stride, 0.0))
        partials.append(
            put_rows(level_out.reshape(picked_rows, head_local, head_size), mask_table, stride, 0.0)
        )
    top_max = reduce(jnp.maximum, maxima)
    factors = [jnp.exp(each_max - top_max) for each_max in maxima]
    total = factors[0] * totals[0]
    summed = factors[0][..., None] * partials[0]
    for level_num in range(1, level_count):
        total = total + factors[level_num] * totals[level_num]
        summed = summed + factors[level_num][..., None] * partials[level_num]
    attended = (summed / total[..., None]).astype(jnp.bfloat16)
    log_total = top_max + jnp.log(total)
    attended_rows_flattened = attended.reshape(tok_rows, -1).astype(jnp.float32)
    first_sum, second_sum = lax.psum(
        (
            jnp.sum(attended_rows_flattened, axis=1),
            jnp.sum(attended_rows_flattened * attended_rows_flattened, axis=1),
        ),
        "head",
    )
    feature_mean = first_sum / feature_total_count
    variance = second_sum / feature_total_count - feature_mean * feature_mean
    inverse_deviation = 1.0 / jnp.sqrt(variance + EPSILON)
    normalized_input = (attended_rows_flattened - feature_mean[:, None]) * inverse_deviation[
        :, None
    ]
    normed = (normalized_input * sublayer_norm_gain[None, :]).astype(jnp.bfloat16)
    normalized_gradient = cotangent.astype(jnp.float32) * sublayer_norm_gain[None, :]
    gradient_sum_first, gradient_sum_second = lax.psum(
        (
            jnp.sum(normalized_gradient, axis=1),
            jnp.sum(normalized_gradient * normalized_input, axis=1),
        ),
        "head",
    )
    attended_gradient = (
        (
            normalized_gradient
            - gradient_sum_first[:, None] / feature_total_count
            - normalized_input * gradient_sum_second[:, None] / feature_total_count
        )
        * inverse_deviation[:, None]
    ).astype(jnp.bfloat16)
    dout_all = attended_gradient.reshape(shape3)
    delta = jnp.sum(dout_all.astype(jnp.float32) * attended.astype(jnp.float32), axis=-1)
    query_acc = jnp.zeros(shape3, jnp.float32)
    key_acc = jnp.zeros(shape3, jnp.float32)
    value_acc = jnp.zeros(shape3, jnp.float32)
    for level_num in range(level_count):
        stride, picked_rows, group_bits, seg_count, mask_table = level_layout(level_num)
        query_sel = pick_rows(query_all, mask_table, stride)
        key_sel = pick_rows(key_all, mask_table, stride)
        value_sel = pick_rows(value_all, mask_table, stride)
        dout_sel = pick_rows(dout_all, mask_table, stride)
        lse_sel = pick_rows(log_total, mask_table, stride)
        delta_sel = pick_rows(delta, mask_table, stride)
        key_group, value_group, query_group = stored[level_num]
        query_seg = query_sel.reshape(seg_count, -1, head_local, head_size)
        dout_seg = dout_sel.reshape(seg_count, -1, head_local, head_size)
        lse_seg = lse_sel.reshape(seg_count, -1, head_local)
        delta_seg = delta_sel.reshape(seg_count, -1, head_local)
        key_seg = key_group.reshape(seg_count, SEG0, head_local, head_size)
        value_seg = value_group.reshape(seg_count, SEG0, head_local, head_size)
        query_part, _, _ = grad_block(
            query_seg, key_seg, value_seg, dout_seg, lse_seg, delta_seg, score_scale, True, False
        )
        dout_group, lse_group, delta_group = gather_rows(
            dout_sel, lse_sel, delta_sel, group_bits, level_num == 0
        )
        _, key_part, value_part = grad_block(
            query_group.reshape(seg_count, SEG0, head_local, head_size),
            key_sel.reshape(seg_count, -1, head_local, head_size),
            value_sel.reshape(seg_count, -1, head_local, head_size),
            dout_group.reshape(seg_count, SEG0, head_local, head_size),
            lse_group.reshape(seg_count, SEG0, head_local),
            delta_group.reshape(seg_count, SEG0, head_local),
            score_scale,
            False,
            True,
        )
        key_own = key_part.reshape(picked_rows, head_local, head_size)
        value_own = value_part.reshape(picked_rows, head_local, head_size)
        query_acc = query_acc + put_rows(
            query_part.reshape(picked_rows, head_local, head_size), mask_table, stride, 0.0
        )
        key_acc = key_acc + put_rows(key_own, mask_table, stride, 0.0)
        value_acc = value_acc + put_rows(value_own, mask_table, stride, 0.0)
    flat_shape = (tok_rows, head_local * head_size)
    query_grad = query_acc.astype(jnp.bfloat16).reshape(flat_shape)
    key_grad = key_acc.astype(jnp.bfloat16).reshape(flat_shape)
    value_grad = value_acc.astype(jnp.bfloat16).reshape(flat_shape)
    return (normed, query_grad, key_grad, value_grad)


def split_mesh(mesh, tok_rows, level_count):
    ctx_count = mesh.shape["ctx"]
    sizes = sorted({max(1, SEG0 * 2**level_num // tok_rows) for level_num in range(level_count)})
    factors = []
    done = 1
    for size in sizes:
        if size > done:
            factors.append(size // done)
            done = size
    factors.append(ctx_count // done)
    names = tuple(f"c{index}" for index in range(len(factors)))
    shape = tuple(reversed(factors)) + (mesh.shape["head"],)
    sub_mesh = jax.sharding.Mesh(
        mesh.devices.reshape(shape), tuple(reversed(names)) + ("head",)
    )
    level_axes = []
    for level_num in range(level_count):
        size = max(1, SEG0 * 2**level_num // tok_rows)
        count = 0
        span = 1
        while span < size:
            span *= factors[count]
            count += 1
        level_axes.append(tuple(reversed(names[:count])))
    return sub_mesh, tuple(reversed(names)), level_axes


def solution(mesh):
    def run(queries, key_rows, value_rows, offsets, sublayer_norm_gain, cotangent):
        tok_rows = queries.shape[0] // mesh.shape["ctx"]
        sub_mesh, ctx_axes, level_axes = split_mesh(mesh, tok_rows, offsets.shape[0])
        rows = P(ctx_axes, "head")
        in_specs = (rows, rows, rows, P(None, "head"), P("head"), rows)
        out_specs = (rows, rows, rows, rows)
        body = partial(on_device, level_axes=level_axes)
        return jax.shard_map(
            body, mesh=sub_mesh, in_specs=in_specs, out_specs=out_specs, check_vma=False
        )(queries, key_rows, value_rows, offsets, sublayer_norm_gain, cotangent)

    return run
```

```python
from functools import partial, reduce
import math

import jax
import jax.numpy as jnp
from jax import lax
from jax.sharding import PartitionSpec as P

SEG0 = 512


NEG_FILL = -1e30
EPSILON = 1e-05


def pick_rows(source, mask_table, stride):
    count = source.shape[0] // stride
    shaped = source.reshape((count, stride) + source.shape[1:])
    chosen = mask_table.reshape((1, stride, mask_table.shape[1]) + (1,) * (source.ndim - 2))
    return jnp.sum(jnp.where(chosen, shaped, jnp.zeros((), source.dtype)), axis=1)


def put_rows(picked, mask_table, stride, filler):
    chosen = mask_table.reshape((1, stride, mask_table.shape[1]) + (1,) * (picked.ndim - 2))
    spread = jnp.where(chosen, picked[:, None], jnp.asarray(filler, picked.dtype))
    return spread.reshape((picked.shape[0] * stride,) + picked.shape[1:])


def exchange(block, group_axes):
    size = 1
    for name in group_axes:
        size *= lax.axis_size(name)
    parts = [block]
    for step in range(1, size):
        parts.append(lax.ppermute(block, group_axes, [(low, low ^ step) for low in range(size)]))
    return jnp.concatenate(parts, 0)


def collect(block, group_axes, direct):
    if direct:
        return exchange(block, group_axes)
    if len(group_axes) > 2:
        block = exchange(block, group_axes[:1])
        group_axes = group_axes[1:]
    return lax.all_gather(block, group_axes, axis=0, tiled=True)


def gather_group(members, group_axes, direct):
    if not group_axes:
        return members
    stacked = jnp.stack(members, axis=1)
    whole = collect(stacked, group_axes, direct)
    return tuple(whole[:, index] for index in range(len(members)))


def split_three(values):
    high = lax.reduce_precision(values, exponent_bits=8, mantissa_bits=7)
    rest = values - high
    middle = lax.reduce_precision(rest, exponent_bits=8, mantissa_bits=7)
    low = rest - middle
    return jnp.stack([high, middle, low], axis=-1).astype(jnp.bfloat16)


def gather_rows(dout_sel, lse_sel, delta_sel, group_axes, direct):
    if not group_axes:
        return (dout_sel, lse_sel, delta_sel)
    rows = dout_sel.shape[0]
    width = dout_sel.shape[1] * dout_sel.shape[2]
    pieces = split_three(jnp.stack([lse_sel, delta_sel], axis=-1))
    flat = jnp.concatenate([dout_sel.reshape(rows, width), pieces.reshape(rows, -1)], axis=1)
    whole = collect(flat, group_axes, direct)
    count = whole.shape[0]
    dout_group = whole[:, :width].reshape((count,) + dout_sel.shape[1:])
    parts = whole[:, width:].reshape((count,) + pieces.shape[1:]).astype(jnp.float32)
    stats = parts[..., 0] + parts[..., 1] + parts[..., 2]
    return (dout_group, stats[..., 0], stats[..., 1])


def grad_block(
    query_seg, key_seg, value_seg, dout_seg, lse_seg, delta_seg, score_scale, want_query, want_keys
):
    lse_t = jnp.transpose(lse_seg, (0, 2, 1))[..., None]
    delta_t = jnp.transpose(delta_seg, (0, 2, 1))[..., None]
    scores = (
        jnp.einsum("sqhd,skhd->shqk", query_seg, key_seg, preferred_element_type=jnp.float32)
        * score_scale
    )
    probs = jnp.exp(scores - lse_t)
    dprobs = jnp.einsum("sqhd,skhd->shqk", dout_seg, value_seg, preferred_element_type=jnp.float32)
    dscores = (probs * (dprobs - delta_t)).astype(jnp.bfloat16)
    query_part = None
    key_part = None
    value_part = None
    if want_query:
        query_part = (
            jnp.einsum("shqk,skhd->sqhd", dscores, key_seg, preferred_element_type=jnp.float32)
            * score_scale
        )
    if want_keys:
        probs_half = probs.astype(jnp.bfloat16)
        key_part = (
            jnp.einsum("shqk,sqhd->skhd", dscores, query_seg, preferred_element_type=jnp.float32)
            * score_scale
        )
        value_part = jnp.einsum(
            "shqk,sqhd->skhd", probs_half, dout_seg, preferred_element_type=jnp.float32
        )
    return (query_part, key_part, value_part)


def on_device(queries, key_rows, value_rows, offsets, sublayer_norm_gain, cotangent, level_axes):
    tok_rows = queries.shape[0]
    head_local = offsets.shape[1]
    head_size = queries.shape[1] // head_local
    level_count = offsets.shape[0]
    feature_total_count = lax.axis_size("head") * queries.shape[1]
    score_scale = 1.0 / math.sqrt(head_size)
    shape3 = (tok_rows, head_local, head_size)
    query_all = queries.reshape(shape3)
    key_all = key_rows.reshape(shape3)
    value_all = value_rows.reshape(shape3)

    def level_layout(level_num):
        stride = 2**level_num
        picked_rows = tok_rows // stride
        group_bits = level_axes[level_num]
        seg_count = max(1, picked_rows // SEG0)
        mask_table = jnp.arange(stride, dtype=jnp.int32)[:, None] == offsets[level_num][None, :]
        return (stride, picked_rows, group_bits, seg_count, mask_table)

    stored = []
    maxima = []
    totals = []
    partials = []
    for level_num in range(level_count):
        stride, picked_rows, group_bits, seg_count, mask_table = level_layout(level_num)
        query_sel = pick_rows(query_all, mask_table, stride)
        key_sel = pick_rows(key_all, mask_table, stride)
        value_sel = pick_rows(value_all, mask_table, stride)
        key_group, value_group, query_group = gather_group(
            (key_sel, value_sel, query_sel), group_bits, level_num == 0
        )
        stored.append((key_group, value_group, query_group))
        query_seg = query_sel.reshape(seg_count, -1, head_local, head_size)
        key_seg = key_group.reshape(seg_count, SEG0, head_local, head_size)
        value_seg = value_group.reshape(seg_count, SEG0, head_local, head_size)
        scores = (
            jnp.einsum("sqhd,skhd->shqk", query_seg, key_seg, preferred_element_type=jnp.float32)
            * score_scale
        )
        row_max = jnp.max(scores, axis=-1)
        weights = jnp.exp(scores - row_max[..., None])
        row_total = jnp.sum(weights, axis=-1)
        level_out = jnp.einsum(
            "shqk,skhd->sqhd",
            weights.astype(jnp.bfloat16),
            value_seg,
            preferred_element_type=jnp.float32,
        )
        flat_max = jnp.transpose(row_max, (0, 2, 1)).reshape(picked_rows, head_local)
        flat_total = jnp.transpose(row_total, (0, 2, 1)).reshape(picked_rows, head_local)
        maxima.append(put_rows(flat_max, mask_table, stride, NEG_FILL))
        totals.append(put_rows(flat_total, mask_table, stride, 0.0))
        partials.append(
            put_rows(level_out.reshape(picked_rows, head_local, head_size), mask_table, stride, 0.0)
        )
    top_max = reduce(jnp.maximum, maxima)
    factors = [jnp.exp(each_max - top_max) for each_max in maxima]
    total = factors[0] * totals[0]
    summed = factors[0][..., None] * partials[0]
    for level_num in range(1, level_count):
        total = total + factors[level_num] * totals[level_num]
        summed = summed + factors[level_num][..., None] * partials[level_num]
    attended = (summed / total[..., None]).astype(jnp.bfloat16)
    log_total = top_max + jnp.log(total)
    attended_rows_flattened = attended.reshape(tok_rows, -1).astype(jnp.float32)
    first_sum, second_sum = lax.psum(
        (
            jnp.sum(attended_rows_flattened, axis=1),
            jnp.sum(attended_rows_flattened * attended_rows_flattened, axis=1),
        ),
        "head",
    )
    feature_mean = first_sum / feature_total_count
    variance = second_sum / feature_total_count - feature_mean * feature_mean
    inverse_deviation = 1.0 / jnp.sqrt(variance + EPSILON)
    normalized_input = (attended_rows_flattened - feature_mean[:, None]) * inverse_deviation[
        :, None
    ]
    normed = (normalized_input * sublayer_norm_gain[None, :]).astype(jnp.bfloat16)
    normalized_gradient = cotangent.astype(jnp.float32) * sublayer_norm_gain[None, :]
    gradient_sum_first, gradient_sum_second = lax.psum(
        (
            jnp.sum(normalized_gradient, axis=1),
            jnp.sum(normalized_gradient * normalized_input, axis=1),
        ),
        "head",
    )
    attended_gradient = (
        (
            normalized_gradient
            - gradient_sum_first[:, None] / feature_total_count
            - normalized_input * gradient_sum_second[:, None] / feature_total_count
        )
        * inverse_deviation[:, None]
    ).astype(jnp.bfloat16)
    dout_all = attended_gradient.reshape(shape3)
    delta = jnp.sum(dout_all.astype(jnp.float32) * attended.astype(jnp.float32), axis=-1)
    query_acc = jnp.zeros(shape3, jnp.float32)
    key_acc = jnp.zeros(shape3, jnp.float32)
    value_acc = jnp.zeros(shape3, jnp.float32)
    for level_num in range(level_count):
        stride, picked_rows, group_bits, seg_count, mask_table = level_layout(level_num)
        query_sel = pick_rows(query_all, mask_table, stride)
        key_sel = pick_rows(key_all, mask_table, stride)
        value_sel = pick_rows(value_all, mask_table, stride)
        dout_sel = pick_rows(dout_all, mask_table, stride)
        lse_sel = pick_rows(log_total, mask_table, stride)
        delta_sel = pick_rows(delta, mask_table, stride)
        key_group, value_group, query_group = stored[level_num]
        query_seg = query_sel.reshape(seg_count, -1, head_local, head_size)
        dout_seg = dout_sel.reshape(seg_count, -1, head_local, head_size)
        lse_seg = lse_sel.reshape(seg_count, -1, head_local)
        delta_seg = delta_sel.reshape(seg_count, -1, head_local)
        key_seg = key_group.reshape(seg_count, SEG0, head_local, head_size)
        value_seg = value_group.reshape(seg_count, SEG0, head_local, head_size)
        query_part, unused_key, unused_value = grad_block(
            query_seg, key_seg, value_seg, dout_seg, lse_seg, delta_seg, score_scale, True, False
        )
        dout_group, lse_group, delta_group = gather_rows(
            dout_sel, lse_sel, delta_sel, group_bits, level_num == 0
        )
        unused_query, key_part, value_part = grad_block(
            query_group.reshape(seg_count, SEG0, head_local, head_size),
            key_sel.reshape(seg_count, -1, head_local, head_size),
            value_sel.reshape(seg_count, -1, head_local, head_size),
            dout_group.reshape(seg_count, SEG0, head_local, head_size),
            lse_group.reshape(seg_count, SEG0, head_local),
            delta_group.reshape(seg_count, SEG0, head_local),
            score_scale,
            False,
            True,
        )
        key_own = key_part.reshape(picked_rows, head_local, head_size)
        value_own = value_part.reshape(picked_rows, head_local, head_size)
        query_acc = query_acc + put_rows(
            query_part.reshape(picked_rows, head_local, head_size), mask_table, stride, 0.0
        )
        key_acc = key_acc + put_rows(key_own, mask_table, stride, 0.0)
        value_acc = value_acc + put_rows(value_own, mask_table, stride, 0.0)
    flat_shape = (tok_rows, head_local * head_size)
    query_grad = query_acc.astype(jnp.bfloat16).reshape(flat_shape)
    key_grad = key_acc.astype(jnp.bfloat16).reshape(flat_shape)
    value_grad = value_acc.astype(jnp.bfloat16).reshape(flat_shape)
    return (normed, query_grad, key_grad, value_grad)


def split_mesh(mesh, tok_rows, level_count):
    ctx_count = mesh.shape["ctx"]
    sizes = sorted({max(1, SEG0 * 2**level_num // tok_rows) for level_num in range(level_count)})
    factors = []
    done = 1
    for size in sizes:
        if size > done:
            factors.append(size // done)
            done = size
    factors.append(ctx_count // done)
    names = tuple(f"c{index}" for index in range(len(factors)))
    shape = tuple(reversed(factors)) + (mesh.shape["head"],)
    sub_mesh = jax.sharding.Mesh(
        mesh.devices.reshape(shape), tuple(reversed(names)) + ("head",)
    )
    level_axes = []
    for level_num in range(level_count):
        size = max(1, SEG0 * 2**level_num // tok_rows)
        count = 0
        span = 1
        while span < size:
            span *= factors[count]
            count += 1
        level_axes.append(tuple(reversed(names[:count])))
    return sub_mesh, tuple(reversed(names)), level_axes


def solution(mesh):
    def run(queries, key_rows, value_rows, offsets, sublayer_norm_gain, cotangent):
        tok_rows = queries.shape[0] // mesh.shape["ctx"]
        sub_mesh, ctx_axes, level_axes = split_mesh(mesh, tok_rows, offsets.shape[0])
        rows = P(ctx_axes, "head")
        in_specs = (rows, rows, rows, P(None, "head"), P("head"), rows)
        out_specs = (rows, rows, rows, rows)
        body = partial(on_device, level_axes=level_axes)
        return jax.shard_map(
            body, mesh=sub_mesh, in_specs=in_specs, out_specs=out_specs, check_vma=False
        )(queries, key_rows, value_rows, offsets, sublayer_norm_gain, cotangent)

    return run
```

```python
from functools import partial, reduce
import math

import jax
import jax.numpy as jnp
from jax import lax
from jax.sharding import PartitionSpec as P

SEG0 = 512


NEG_FILL = -1e30
EPSILON = 1e-05


def pick_rows(source, mask_table, stride):
    count = source.shape[0] // stride
    shaped = source.reshape((count, stride) + source.shape[1:])
    chosen = mask_table.reshape((1, stride, mask_table.shape[1]) + (1,) * (source.ndim - 2))
    return jnp.sum(jnp.where(chosen, shaped, jnp.zeros((), source.dtype)), axis=1)


def put_rows(picked, mask_table, stride, filler):
    chosen = mask_table.reshape((1, stride, mask_table.shape[1]) + (1,) * (picked.ndim - 2))
    spread = jnp.where(chosen, picked[:, None], jnp.asarray(filler, picked.dtype))
    return spread.reshape((picked.shape[0] * stride,) + picked.shape[1:])


def exchange(block, group_axes):
    size = 1
    for name in group_axes:
        size *= lax.axis_size(name)
    parts = [block]
    for step in range(1, size):
        parts.append(lax.ppermute(block, group_axes, [(low, low ^ step) for low in range(size)]))
    return jnp.concatenate(parts, 0)


def collect(block, group_axes, direct):
    if direct:
        return exchange(block, group_axes)
    if len(group_axes) > 2:
        block = exchange(block, group_axes[:1])
        group_axes = group_axes[1:]
    return lax.all_gather(block, group_axes, axis=0, tiled=True)


def gather_group(members, group_axes, direct):
    if not group_axes:
        return members
    stacked = jnp.stack(members, axis=1)
    whole = collect(stacked, group_axes, direct)
    return tuple(whole[:, index] for index in range(len(members)))


def split_three(values):
    high = lax.reduce_precision(values, exponent_bits=8, mantissa_bits=7)
    low = values - high
    return jnp.stack([high, low], axis=-1).astype(jnp.bfloat16)


def gather_rows(dout_sel, lse_sel, delta_sel, group_axes, direct):
    if not group_axes:
        return (dout_sel, lse_sel, delta_sel)
    rows = dout_sel.shape[0]
    width = dout_sel.shape[1] * dout_sel.shape[2]
    pieces = split_three(jnp.stack([lse_sel, delta_sel], axis=-1))
    flat = jnp.concatenate([dout_sel.reshape(rows, width), pieces.reshape(rows, -1)], axis=1)
    whole = collect(flat, group_axes, direct)
    count = whole.shape[0]
    dout_group = whole[:, :width].reshape((count,) + dout_sel.shape[1:])
    parts = whole[:, width:].reshape((count,) + pieces.shape[1:]).astype(jnp.float32)
    stats = parts[..., 0] + parts[..., 1]
    return (dout_group, stats[..., 0], stats[..., 1])


def grad_block(
    query_seg, key_seg, value_seg, dout_seg, lse_seg, delta_seg, score_scale, want_query, want_keys
):
    lse_t = jnp.transpose(lse_seg, (0, 2, 1))[..., None]
    delta_t = jnp.transpose(delta_seg, (0, 2, 1))[..., None]
    scores = (
        jnp.einsum("sqhd,skhd->shqk", query_seg, key_seg, preferred_element_type=jnp.float32)
        * score_scale
    )
    probs = jnp.exp(scores - lse_t)
    dprobs = jnp.einsum("sqhd,skhd->shqk", dout_seg, value_seg, preferred_element_type=jnp.float32)
    dscores = (probs * (dprobs - delta_t)).astype(jnp.bfloat16)
    query_part = None
    key_part = None
    value_part = None
    if want_query:
        query_part = (
            jnp.einsum("shqk,skhd->sqhd", dscores, key_seg, preferred_element_type=jnp.float32)
            * score_scale
        )
    if want_keys:
        probs_half = probs.astype(jnp.bfloat16)
        key_part = (
            jnp.einsum("shqk,sqhd->skhd", dscores, query_seg, preferred_element_type=jnp.float32)
            * score_scale
        )
        value_part = jnp.einsum(
            "shqk,sqhd->skhd", probs_half, dout_seg, preferred_element_type=jnp.float32
        )
    return (query_part, key_part, value_part)


def on_device(queries, key_rows, value_rows, offsets, sublayer_norm_gain, cotangent, level_axes):
    tok_rows = queries.shape[0]
    head_local = offsets.shape[1]
    head_size = queries.shape[1] // head_local
    level_count = offsets.shape[0]
    feature_total_count = lax.axis_size("head") * queries.shape[1]
    score_scale = 1.0 / math.sqrt(head_size)
    shape3 = (tok_rows, head_local, head_size)
    query_all = queries.reshape(shape3)
    key_all = key_rows.reshape(shape3)
    value_all = value_rows.reshape(shape3)

    def level_layout(level_num):
        stride = 2**level_num
        picked_rows = tok_rows // stride
        group_bits = level_axes[level_num]
        seg_count = max(1, picked_rows // SEG0)
        mask_table = jnp.arange(stride, dtype=jnp.int32)[:, None] == offsets[level_num][None, :]
        return (stride, picked_rows, group_bits, seg_count, mask_table)

    stored = []
    maxima = []
    totals = []
    partials = []
    for level_num in range(level_count):
        stride, picked_rows, group_bits, seg_count, mask_table = level_layout(level_num)
        query_sel = pick_rows(query_all, mask_table, stride)
        key_sel = pick_rows(key_all, mask_table, stride)
        value_sel = pick_rows(value_all, mask_table, stride)
        key_group, value_group, query_group = gather_group(
            (key_sel, value_sel, query_sel), group_bits, level_num == 0
        )
        stored.append((key_group, value_group, query_group))
        query_seg = query_sel.reshape(seg_count, -1, head_local, head_size)
        key_seg = key_group.reshape(seg_count, SEG0, head_local, head_size)
        value_seg = value_group.reshape(seg_count, SEG0, head_local, head_size)
        scores = (
            jnp.einsum("sqhd,skhd->shqk", query_seg, key_seg, preferred_element_type=jnp.float32)
            * score_scale
        )
        row_max = jnp.max(scores, axis=-1)
        weights = jnp.exp(scores - row_max[..., None])
        row_total = jnp.sum(weights, axis=-1)
        level_out = jnp.einsum(
            "shqk,skhd->sqhd",
            weights.astype(jnp.bfloat16),
            value_seg,
            preferred_element_type=jnp.float32,
        )
        flat_max = jnp.transpose(row_max, (0, 2, 1)).reshape(picked_rows, head_local)
        flat_total = jnp.transpose(row_total, (0, 2, 1)).reshape(picked_rows, head_local)
        maxima.append(put_rows(flat_max, mask_table, stride, NEG_FILL))
        totals.append(put_rows(flat_total, mask_table, stride, 0.0))
        partials.append(
            put_rows(level_out.reshape(picked_rows, head_local, head_size), mask_table, stride, 0.0)
        )
    top_max = reduce(jnp.maximum, maxima)
    factors = [jnp.exp(each_max - top_max) for each_max in maxima]
    total = factors[0] * totals[0]
    summed = factors[0][..., None] * partials[0]
    for level_num in range(1, level_count):
        total = total + factors[level_num] * totals[level_num]
        summed = summed + factors[level_num][..., None] * partials[level_num]
    attended = (summed / total[..., None]).astype(jnp.bfloat16)
    log_total = top_max + jnp.log(total)
    attended_rows_flattened = attended.reshape(tok_rows, -1).astype(jnp.float32)
    first_sum, second_sum = lax.psum(
        (
            jnp.sum(attended_rows_flattened, axis=1),
            jnp.sum(attended_rows_flattened * attended_rows_flattened, axis=1),
        ),
        "head",
    )
    feature_mean = first_sum / feature_total_count
    variance = second_sum / feature_total_count - feature_mean * feature_mean
    inverse_deviation = 1.0 / jnp.sqrt(variance + EPSILON)
    normalized_input = (attended_rows_flattened - feature_mean[:, None]) * inverse_deviation[
        :, None
    ]
    normed = (normalized_input * sublayer_norm_gain[None, :]).astype(jnp.bfloat16)
    normalized_gradient = cotangent.astype(jnp.float32) * sublayer_norm_gain[None, :]
    gradient_sum_first, gradient_sum_second = lax.psum(
        (
            jnp.sum(normalized_gradient, axis=1),
            jnp.sum(normalized_gradient * normalized_input, axis=1),
        ),
        "head",
    )
    attended_gradient = (
        (
            normalized_gradient
            - gradient_sum_first[:, None] / feature_total_count
            - normalized_input * gradient_sum_second[:, None] / feature_total_count
        )
        * inverse_deviation[:, None]
    ).astype(jnp.bfloat16)
    dout_all = attended_gradient.reshape(shape3)
    delta = jnp.sum(dout_all.astype(jnp.float32) * attended.astype(jnp.float32), axis=-1)
    query_acc = jnp.zeros(shape3, jnp.float32)
    key_acc = jnp.zeros(shape3, jnp.float32)
    value_acc = jnp.zeros(shape3, jnp.float32)
    for level_num in range(level_count):
        stride, picked_rows, group_bits, seg_count, mask_table = level_layout(level_num)
        query_sel = pick_rows(query_all, mask_table, stride)
        key_sel = pick_rows(key_all, mask_table, stride)
        value_sel = pick_rows(value_all, mask_table, stride)
        dout_sel = pick_rows(dout_all, mask_table, stride)
        lse_sel = pick_rows(log_total, mask_table, stride)
        delta_sel = pick_rows(delta, mask_table, stride)
        key_group, value_group, query_group = stored[level_num]
        query_seg = query_sel.reshape(seg_count, -1, head_local, head_size)
        dout_seg = dout_sel.reshape(seg_count, -1, head_local, head_size)
        lse_seg = lse_sel.reshape(seg_count, -1, head_local)
        delta_seg = delta_sel.reshape(seg_count, -1, head_local)
        key_seg = key_group.reshape(seg_count, SEG0, head_local, head_size)
        value_seg = value_group.reshape(seg_count, SEG0, head_local, head_size)
        query_part, unused_key, unused_value = grad_block(
            query_seg, key_seg, value_seg, dout_seg, lse_seg, delta_seg, score_scale, True, False
        )
        dout_group, lse_group, delta_group = gather_rows(
            dout_sel, lse_sel, delta_sel, group_bits, level_num == 0
        )
        unused_query, key_part, value_part = grad_block(
            query_group.reshape(seg_count, SEG0, head_local, head_size),
            key_sel.reshape(seg_count, -1, head_local, head_size),
            value_sel.reshape(seg_count, -1, head_local, head_size),
            dout_group.reshape(seg_count, SEG0, head_local, head_size),
            lse_group.reshape(seg_count, SEG0, head_local),
            delta_group.reshape(seg_count, SEG0, head_local),
            score_scale,
            False,
            True,
        )
        key_own = key_part.reshape(picked_rows, head_local, head_size)
        value_own = value_part.reshape(picked_rows, head_local, head_size)
        query_acc = query_acc + put_rows(
            query_part.reshape(picked_rows, head_local, head_size), mask_table, stride, 0.0
        )
        key_acc = key_acc + put_rows(key_own, mask_table, stride, 0.0)
        value_acc = value_acc + put_rows(value_own, mask_table, stride, 0.0)
    flat_shape = (tok_rows, head_local * head_size)
    query_grad = query_acc.astype(jnp.bfloat16).reshape(flat_shape)
    key_grad = key_acc.astype(jnp.bfloat16).reshape(flat_shape)
    value_grad = value_acc.astype(jnp.bfloat16).reshape(flat_shape)
    return (normed, query_grad, key_grad, value_grad)


def split_mesh(mesh, tok_rows, level_count):
    ctx_count = mesh.shape["ctx"]
    sizes = sorted({max(1, SEG0 * 2**level_num // tok_rows) for level_num in range(level_count)})
    factors = []
    done = 1
    for size in sizes:
        if size > done:
            factors.append(size // done)
            done = size
    factors.append(ctx_count // done)
    names = tuple(f"c{index}" for index in range(len(factors)))
    shape = tuple(reversed(factors)) + (mesh.shape["head"],)
    sub_mesh = jax.sharding.Mesh(
        mesh.devices.reshape(shape), tuple(reversed(names)) + ("head",)
    )
    level_axes = []
    for level_num in range(level_count):
        size = max(1, SEG0 * 2**level_num // tok_rows)
        count = 0
        span = 1
        while span < size:
            span *= factors[count]
            count += 1
        level_axes.append(tuple(reversed(names[:count])))
    return sub_mesh, tuple(reversed(names)), level_axes


def solution(mesh):
    def run(queries, key_rows, value_rows, offsets, sublayer_norm_gain, cotangent):
        tok_rows = queries.shape[0] // mesh.shape["ctx"]
        sub_mesh, ctx_axes, level_axes = split_mesh(mesh, tok_rows, offsets.shape[0])
        rows = P(ctx_axes, "head")
        in_specs = (rows, rows, rows, P(None, "head"), P("head"), rows)
        out_specs = (rows, rows, rows, rows)
        body = partial(on_device, level_axes=level_axes)
        return jax.shard_map(
            body, mesh=sub_mesh, in_specs=in_specs, out_specs=out_specs, check_vma=False
        )(queries, key_rows, value_rows, offsets, sublayer_norm_gain, cotangent)

    return run
```
